512 devices in a mesh: freq: 16 (over z, core), row: 32 (over x, y).
Axes of the slice: x: 4, y: 8, z: 8, core: 2. Of those that a mesh axis runs over, the one named last changes fastest.
Arguments:
- vis_values: bfloat16 [16, 2048, 2, 128], P('freq', 'row'), may hold values from -6 to 6
- kernel_u: bfloat16 [16, 2048, 7, 128], P('freq', 'row'), may hold values from 0.049804688 to 1
- kernel_v: bfloat16 [16, 2048, 7, 128], P('freq', 'row'), may hold values from 0.049804688 to 1
- offset_u: int32 [16, 2048, 128], P('freq', 'row'), may hold values from 0 to 9
- offset_v: int32 [16, 2048, 128], P('freq', 'row'), may hold values from 0 to 121
- block_owner: int32 [16, 2048, 1], P('freq', 'row'), may hold values from 0 to 31; in each aligned block of 64 rows (0 to 63, 64 to 127, ..., all dimensions but the last counted through in order) at most 8 rows name the same one
- tile_slot: int32 [16, 2048], P('freq', 'row'), may hold values from 0 to 255
- channel_freq: float32 [16], P('freq'), may hold values from 0.856 to 1.712
Outputs:
- taylor: bfloat16 [3, 4096, 4096], P(None, 'freq', 'row')
The draws below stay inside these ranges and needn't reach their ends.
Inputs may be any that keep to these rules, and one draw needn't show every extreme that they name: `block_owner`: among the 64 blocks of one channel held by one index of row, at most 8 name the same owner, a bound that some block reaches.
All inputs are finite; a program needn't handle non-finite values.
Results may differ from the reference program's by a relative error of at most 0.024.
Values may be sent and summed in bfloat16 or wider, within the bound.
No kernel may reach another device: no remote copies, remote signals or barrier semaphores. Data moves between devices by JAX's collectives and lax.ppermute only.
A program may use at most 64 MiB of HBM per device.

```python
import math
import jax
import jax.numpy as jnp
import numpy as np
from jax import lax

GRID = 4096
TU = 16
TV = 128
TAPS = 7
BV = 128
NBLK = 64
CHANNELS = 16
BLOCKS = 2048
CAP = 8
TS = 256
N_ROW = 32


def touch_ends(values, stream_key, smallest, high):
    longest = values.shape.index(max(values.shape))
    spots = []
    for shift in (0, 1):
        where = [jax.random.randint(jax.random.fold_in(stream_key, axis), (), 0, length) for axis, length in enumerate(values.shape)]
        where[longest] = (where[longest] + shift) % values.shape[longest]
        spots.append(tuple(where))
    return values.at[spots[0]].set(smallest).at[spots[1]].set(high)


def steps_of(stream_key, extent, cuts, smallest, top_value):
    factor_of = 1.0
    for dim, parts in cuts:
        steps = jax.random.uniform(jax.random.fold_in(jax.random.fold_in(stream_key, 6), dim), (parts,), jnp.float32, smallest / len(cuts), top_value / len(cuts))
        factor_of = factor_of * jnp.repeat(jnp.exp(steps), extent[dim] // parts).reshape((-1,) + (1,) * (len(extent) - 1 - dim))
    return factor_of


def deal_out(own_key, own, number, rows, number_of, top, bound, skew):
    ranking = jax.random.permutation(own_key, number_of)
    heavy_load, common = portions_of(number_of, rows * top, bound, skew, True), portions_of(number_of, rows * top, bound, skew, False)
    places = jnp.arange(number_of)

    def named(tallies, rotation):
        used = int((tallies > 0).sum())
        fixed = max(1, used // 4)
        passed = fixed + (places - fixed + rotation * (used - fixed)) % max(1, number_of - fixed)
        return jnp.zeros((number_of,), jnp.int32).at[ranking[jnp.where(places < fixed, places, passed)]].set(jnp.asarray(tallies, jnp.int32))

    tallies = jnp.where(number % 4 == 0, named(heavy_load, number // 4), named(common, number - number // 4 - 1))
    mixed = jax.random.permutation(jax.random.fold_in(own, 3), number_of)
    source_of, receiver = mixed[0:number_of // 2 * 2:2], mixed[1:number_of // 2 * 2:2]
    slack = jnp.minimum(tallies[source_of] - 1, bound - tallies[receiver]) // 2
    slack = jnp.where((source_of == ranking[0]) | (receiver == ranking[0]) | (tallies[receiver] == 0), 0, jnp.maximum(slack, 0))
    passed = jax.random.randint(jax.random.fold_in(own, 4), (number_of // 2,), 0, 1 << 20) % (slack + 1)
    tallies = tallies.at[source_of].add(-passed).at[receiver].add(passed)
    items = jnp.searchsorted(jnp.cumsum(tallies), jnp.arange(rows * top), side="right").astype(jnp.int32)
    grid = items.reshape(top, rows).T
    grid = grid[jax.random.permutation(jax.random.fold_in(own, 1), rows)]
    rotation = jax.random.randint(jax.random.fold_in(own, 2), (rows, 1), 0, top)
    return jnp.take_along_axis(grid, (jnp.arange(top)[None, :] + rotation) % top, axis=1)


def portions_of(number_of, total, reach, lean, full):
    weights = [(1 << 20) // math.isqrt(grade ** lean) + 1 for grade in range(1, number_of + 1)]
    largest = reach if full else min(reach, max(-(-total // number_of), total * weights[0] // sum(weights)))
    least = 1 if total - largest >= number_of - 1 else 0
    counts, surplus = [largest] + [least] * (number_of - 1), total - largest - least * (number_of - 1)
    while surplus > 0:
        candidates = [i for i in range(1, number_of) if counts[i] < largest] or [i for i in range(1, number_of) if counts[i] < reach]
        mass, remaining = sum([weights[i] for i in candidates]), surplus
        for i in candidates:
            extra = min(reach - counts[i], max(1, remaining * weights[i] // mass), surplus)
            counts[i] = counts[i] + extra
            surplus = surplus - extra
    return np.array(counts)


def bell_draw(own_key, extent, width, most, cuts=(), held_as=jnp.bfloat16):
    drawn = jax.random.normal(own_key, extent, jnp.float32) * width
    if len(cuts) > 0:
        drawn = steps_of(own_key, extent, cuts, -0.22, 0.18) * drawn
    return jnp.clip(drawn, min=-most, max=most).astype(held_as)


def setup_inputs(seed: int = 0) -> dict:
    key_of = jax.random.split(jax.random.key(seed), 9)
    vis_values = bell_draw(key_of[0], (CHANNELS, BLOCKS, 2, BV), 1.0, 6.0, ((0, 16), (1, 32)))
    kernel_u = jnp.clip(jnp.exp(math.log(1.0) - 2.9996462 * jax.random.uniform(key_of[1], (CHANNELS, BLOCKS, TAPS, BV), jnp.float32) ** steps_of(key_of[1], (CHANNELS, BLOCKS, TAPS, BV), ((0, 16), (1, 32)), -0.2, 0.2)), 0.049804688, 1.0).astype(jnp.bfloat16)
    kernel_v = jnp.clip(jnp.exp(math.log(1.0) - 2.9996462 * jax.random.uniform(key_of[2], (CHANNELS, BLOCKS, TAPS, BV), jnp.float32) ** steps_of(key_of[2], (CHANNELS, BLOCKS, TAPS, BV), ((0, 16), (1, 32)), -0.2, 0.2)), 0.049804688, 1.0).astype(jnp.bfloat16)
    offset_u = touch_ends(jax.random.randint(key_of[3], (CHANNELS, BLOCKS, BV), 0, TU - TAPS + 1), jax.random.fold_in(key_of[3], 1), 0, TU - TAPS).astype(jnp.int32)
    offset_v = touch_ends(jax.random.randint(key_of[4], (CHANNELS, BLOCKS, BV), 0, TV - TAPS + 1), jax.random.fold_in(key_of[4], 1), 0, TV - TAPS).astype(jnp.int32)
    block_owner_keys = jax.random.split(jax.random.fold_in(key_of[5], 1), CHANNELS * BLOCKS // NBLK)
    block_owner_turns = jax.random.permutation(jax.random.fold_in(key_of[5], 3), CHANNELS * BLOCKS // NBLK)
    block_owner = jax.vmap(lambda own, number: deal_out(jax.random.fold_in(key_of[5], 2), own, number, NBLK, N_ROW, 1, CAP, 2))(block_owner_keys, block_owner_turns).reshape((CHANNELS, BLOCKS, 1))
    tile_slot = touch_ends(jax.random.randint(key_of[6], (CHANNELS, BLOCKS), 0, TS), jax.random.fold_in(key_of[6], 1), 0, TS - 1).astype(jnp.int32)
    channel_freq = jnp.clip(0.856 + 0.856 * jax.random.uniform(key_of[7], (CHANNELS,), jnp.float32) ** steps_of(key_of[7], (CHANNELS,), ((0, 16),), -0.2, 0.2), 0.856, 1.712)
    return {"vis_values": vis_values, "kernel_u": kernel_u, "kernel_v": kernel_v, "offset_u": offset_u, "offset_v": offset_v, "block_owner": block_owner, "tile_slot": tile_slot, "channel_freq": channel_freq}


def grid_channel(vis, kern_u, kern_v, offs_u, offs_v):
    row_grid = jnp.arange(TU, dtype=jnp.int32)[None, :, None]
    col_grid = jnp.arange(TV, dtype=jnp.int32)[None, None, :]
    spread_u = jnp.zeros((vis.shape[0], TU, BV), jnp.float32)
    spread_v = jnp.zeros((vis.shape[0], BV, TV), jnp.float32)
    for tap_index in range(TAPS):
        spread_u = spread_u + jnp.where(row_grid == offs_u[:, None, :] + tap_index, kern_u[:, tap_index:tap_index + 1, :].astype(jnp.float32), 0.0)
        spread_v = spread_v + jnp.where(col_grid == offs_v[:, :, None] + tap_index, kern_v[:, tap_index, :, None].astype(jnp.float32), 0.0)
    left = (vis.astype(jnp.float32)[:, :, None, :] * spread_u[:, None, :, :]).astype(jnp.bfloat16)
    left = lax.optimization_barrier(left)
    return jnp.einsum('bpin,bnj->bpij', left.astype(jnp.float32), spread_v)

def reference(vis_values, kernel_u, kernel_v, offset_u, offset_v, block_owner, tile_slot, channel_freq):
    tiles_slab = GRID // N_ROW // TU * (GRID // TV)
    image_scale = 1.0 / math.sqrt(BLOCKS * BV)

    def one_channel(total, inputs):
        vis, kern_u, kern_v, offs_u, offs_v, owner_row, slot_row, frequency = inputs
        contribution = grid_channel(vis, kern_u, kern_v, offs_u, offs_v)
        tile_ids = (owner_row[:, 0] * tiles_slab + slot_row).astype(jnp.int32)
        tiles_all = jnp.zeros((N_ROW * tiles_slab, 2, TU, TV), jnp.float32).at[tile_ids].add(contribution)
        uv_grid = tiles_all.reshape(GRID // TU, GRID // TV, 2, TU, TV).transpose(2, 0, 3, 1, 4).reshape(2, GRID, GRID)
        field = lax.complex(uv_grid[0], uv_grid[1])
        dirty_image = jnp.real(jnp.fft.ifft2(field)) * (GRID * GRID * image_scale)
        offset_freq = (frequency - 1.284) / 0.428
        weights = jnp.stack([jnp.ones_like(offset_freq), offset_freq, offset_freq * offset_freq])
        taylor_terms = (weights[:, None, None] * dirty_image[None]).astype(jnp.bfloat16)
        return (total + taylor_terms.astype(jnp.float32), None)
    start = jnp.zeros((3, GRID, GRID), jnp.float32)
    total, _ = lax.scan(one_channel, start, (vis_values, kernel_u, kernel_v, offset_u, offset_v, block_owner, tile_slot, channel_freq))
    return total.astype(jnp.bfloat16)
```

```python
from functools import partial
import math

import jax
import jax.numpy as jnp
from jax import lax
from jax.sharding import PartitionSpec as P
from jax.experimental import pallas as pl
from jax.experimental.pallas import tpu as pltpu

GRID = 4096
TU = 16
TV = 128


def for_sending(shard):
    return jax.tree.map(lambda a: a.astype(jnp.bfloat16) if a.dtype == jnp.float32 else a, shard)


def dft_tables(length):
    outer_len = 32
    inner_len = length // outer_len
    index_outer = jnp.arange(outer_len, dtype=jnp.int32)
    index_inner = jnp.arange(inner_len, dtype=jnp.int32)
    full_turn = 2.0 * math.pi
    angle_outer = (
        full_turn
        * (index_outer[:, None] * index_outer[None, :] % outer_len).astype(jnp.float32)
        / outer_len
    )
    angle_twist = (
        full_turn
        * (index_outer[:, None] * index_inner[None, :] % length).astype(jnp.float32)
        / length
    )
    angle_inner = (
        full_turn
        * (index_inner[:, None] * index_inner[None, :] % inner_len).astype(jnp.float32)
        / inner_len
    )
    return (
        jnp.cos(angle_outer),
        jnp.sin(angle_outer),
        jnp.cos(angle_twist),
        jnp.sin(angle_twist),
        jnp.cos(angle_inner),
        jnp.sin(angle_inner),
    )


def transform_last(real_part, imag_part):
    row_total, length = real_part.shape
    outer_len = 32
    inner_len = length // outer_len
    cos_outer, sin_outer, cos_twist, sin_twist, cos_inner, sin_inner = dft_tables(length)
    product = partial(jnp.einsum, precision=lax.Precision.HIGHEST)
    real_part = real_part.reshape(row_total, outer_len, inner_len)
    imag_part = imag_part.reshape(row_total, outer_len, inner_len)
    step_real = product("rab,ak->rkb", real_part, cos_outer) - product(
        "rab,ak->rkb", imag_part, sin_outer
    )
    step_imag = product("rab,ak->rkb", real_part, sin_outer) + product(
        "rab,ak->rkb", imag_part, cos_outer
    )
    twist_real = step_real * cos_twist - step_imag * sin_twist
    twist_imag = step_real * sin_twist + step_imag * cos_twist
    out_real = product("rkb,bm->rmk", twist_real, cos_inner) - product(
        "rkb,bm->rmk", twist_imag, sin_inner
    )
    out_imag = product("rkb,bm->rmk", twist_real, sin_inner) + product(
        "rkb,bm->rmk", twist_imag, cos_inner
    )
    return (out_real.reshape(row_total, length), out_imag.reshape(row_total, length))


def transform_first_real(real_part, imag_part):
    length, col_total = real_part.shape
    outer_len = 32
    inner_len = length // outer_len
    cos_outer, sin_outer, cos_twist, sin_twist, cos_inner, sin_inner = dft_tables(length)
    product = partial(jnp.einsum, precision=lax.Precision.HIGHEST)
    real_part = real_part.reshape(outer_len, inner_len, col_total)
    imag_part = imag_part.reshape(outer_len, inner_len, col_total)
    step_real = product("abc,ak->kbc", real_part, cos_outer) - product(
        "abc,ak->kbc", imag_part, sin_outer
    )
    step_imag = product("abc,ak->kbc", real_part, sin_outer) + product(
        "abc,ak->kbc", imag_part, cos_outer
    )
    twist_real = step_real * cos_twist[:, :, None] - step_imag * sin_twist[:, :, None]
    twist_imag = step_real * sin_twist[:, :, None] + step_imag * cos_twist[:, :, None]
    out_real = product("kbc,bm->mkc", twist_real, cos_inner) - product(
        "kbc,bm->mkc", twist_imag, sin_inner
    )
    return out_real.reshape(length, col_total)


PAY_ROWS = 19


def grid_kernel(tile_ref, pay_ref, out_ref):
    tiles_total = out_ref.shape[1] // TU * (out_ref.shape[2] // TV)
    tile_cols = out_ref.shape[2] // TV
    out_ref[...] = jnp.zeros(out_ref.shape, jnp.float32)

    def body(b, carry):
        tile = tile_ref[b]

        @pl.when(tile < tiles_total)
        def _():
            blk = pay_ref[b].astype(jnp.float32)
            vis = blk[0:2]
            ku = blk[2:9]
            kv = blk[9:16]
            ou = blk[16:17].astype(jnp.int32)
            ov = blk[17:18].astype(jnp.int32)
            du = lax.broadcasted_iota(jnp.int32, (TU, blk.shape[1]), 0) - ou
            su = jnp.zeros((TU, blk.shape[1]), jnp.float32)
            for t in range(7):
                su = jnp.where(du == t, ku[t : t + 1], su)
            left = jnp.concatenate([vis[0:1] * su, vis[1:2] * su], axis=0).astype(jnp.bfloat16)
            dv = lax.broadcasted_iota(jnp.int32, (TV, blk.shape[1]), 0) - ov
            sv = jnp.zeros((TV, blk.shape[1]), jnp.float32)
            for t in range(7):
                sv = jnp.where(dv == t, kv[t : t + 1], sv)
            sv = sv.astype(jnp.bfloat16)
            contrib = lax.dot_general(
                left, sv, (((1,), (1,)), ((), ())), preferred_element_type=jnp.float32
            )
            row0 = pl.multiple_of((tile // tile_cols) * TU, TU)
            col0 = pl.multiple_of((tile % tile_cols) * TV, TV)
            for p in range(2):
                out_ref[p, pl.ds(row0, TU), pl.ds(col0, TV)] += contrib[p * TU : (p + 1) * TU]

        return carry

    lax.fori_loop(0, pay_ref.shape[0], body, 0)


def grid_into_slab(tile_ids, payload, slab_rows):
    return pl.pallas_call(
        grid_kernel,
        out_shape=jax.ShapeDtypeStruct((2, slab_rows, GRID), jnp.float32),
        in_specs=[
            pl.BlockSpec(memory_space=pltpu.SMEM),
            pl.BlockSpec(memory_space=pltpu.VMEM),
        ],
        out_specs=pl.BlockSpec(memory_space=pltpu.VMEM),
    )(tile_ids, payload)


def shards(
    vis_values, kernel_u, kernel_v, offset_u, offset_v, block_owner, tile_slot, channel_freq
):
    row_count = lax.axis_size("row")
    block_count = vis_values.shape[1]
    vis_count = vis_values.shape[3]
    capacity = max(2, 4 * block_count // row_count)
    slot_count = row_count * capacity
    slab_rows = GRID // row_count
    tiles_total = slab_rows // TU * (GRID // TV)
    owner_row = block_owner[0, :, 0]
    row_marks = (owner_row[:, None] == jnp.arange(row_count, dtype=jnp.int32)[None, :]).astype(
        jnp.int32
    )
    before = jnp.cumsum(row_marks, axis=0) - row_marks
    slot_rank = jnp.sum(before * row_marks, axis=1)
    target = owner_row * capacity + slot_rank
    tile_row = jnp.broadcast_to(
        tile_slot[0][:, None, None].astype(jnp.bfloat16), (block_count, 1, vis_count)
    )
    payload = jnp.concatenate(
        [
            vis_values[0],
            kernel_u[0],
            kernel_v[0],
            offset_u[0][:, None, :].astype(jnp.bfloat16),
            offset_v[0][:, None, :].astype(jnp.bfloat16),
            tile_row,
        ],
        axis=1,
    )
    pick = (target[None, :] == jnp.arange(slot_count, dtype=jnp.int32)[:, None]).astype(
        jnp.bfloat16
    )
    send = jnp.einsum(
        "sb,bkn->skn", pick, payload, preferred_element_type=jnp.float32
    )
    empty = 1.0 - jnp.sum(pick.astype(jnp.float32), axis=1)
    send = send.at[:, PAY_ROWS - 1, :].add(empty[:, None] * tiles_total)
    send = send.astype(jnp.bfloat16)
    recv = lax.all_to_all(
        send.reshape((row_count, capacity) + payload.shape[1:]),
        "row",
        split_axis=0,
        concat_axis=0,
        tiled=True,
    ).reshape((slot_count,) + payload.shape[1:])
    tile_ids = recv[:, PAY_ROWS - 1, 0].astype(jnp.int32)
    slab_grid = grid_into_slab(tile_ids, recv, slab_rows)
    spec_real, spec_imag = transform_last(slab_grid[0], slab_grid[1])
    spectrum = jnp.stack([spec_real, spec_imag]).reshape(2, slab_rows, row_count, GRID // row_count)
    image_scale = 1.0 / math.sqrt(block_count * row_count * vis_count)
    offset_freq = (channel_freq[0] - 1.284) / 0.428
    weights = jnp.stack([jnp.ones_like(offset_freq), offset_freq, offset_freq * offset_freq])
    received = lax.all_to_all(
        for_sending(spectrum), "row", split_axis=2, concat_axis=1, tiled=True
    ).astype(spectrum.dtype)
    width_here = received.shape[2] * received.shape[3]
    real_cols = received[0].reshape(GRID, width_here)
    imag_cols = received[1].reshape(GRID, width_here)
    dirty_image = transform_first_real(real_cols, imag_cols) * image_scale
    taylor_terms = (weights[:, None, None] * dirty_image[None]).astype(jnp.bfloat16)
    terms_all = taylor_terms.reshape(3, GRID, received.shape[2], received.shape[3])
    terms_all = terms_all.reshape(3, GRID, GRID // row_count).astype(jnp.float32)
    summed = lax.psum_scatter(
        terms_all.astype(jnp.bfloat16), "freq", scatter_dimension=1, tiled=True
    )
    return summed


def solution(mesh):
    return jax.shard_map(
        shards,
        mesh=mesh,
        in_specs=(
            P("freq", "row", None, None),
            P("freq", "row", None, None),
            P("freq", "row", None, None),
            P("freq", "row", None),
            P("freq", "row", None),
            P("freq", "row", None),
            P("freq", "row"),
            P("freq"),
        ),
        out_specs=P(None, "freq", "row"),
        check_vma=False,
    )
```

```python
from functools import partial
import math

import jax
import jax.numpy as jnp
from jax import lax
from jax.sharding import PartitionSpec as P
from jax.experimental import pallas as pl
from jax.experimental.pallas import tpu as pltpu

GRID = 4096
TU = 16
TV = 128


def for_sending(shard):
    return jax.tree.map(lambda a: a.astype(jnp.bfloat16) if a.dtype == jnp.float32 else a, shard)


def dft_tables(length):
    outer_len = 32
    inner_len = length // outer_len
    index_outer = jnp.arange(outer_len, dtype=jnp.int32)
    index_inner = jnp.arange(inner_len, dtype=jnp.int32)
    full_turn = 2.0 * math.pi
    angle_outer = (
        full_turn
        * (index_outer[:, None] * index_outer[None, :] % outer_len).astype(jnp.float32)
        / outer_len
    )
    angle_twist = (
        full_turn
        * (index_outer[:, None] * index_inner[None, :] % length).astype(jnp.float32)
        / length
    )
    angle_inner = (
        full_turn
        * (index_inner[:, None] * index_inner[None, :] % inner_len).astype(jnp.float32)
        / inner_len
    )
    return (
        jnp.cos(angle_outer),
        jnp.sin(angle_outer),
        jnp.cos(angle_twist),
        jnp.sin(angle_twist),
        jnp.cos(angle_inner),
        jnp.sin(angle_inner),
    )


def transform_last(real_part, imag_part):
    row_total, length = real_part.shape
    outer_len = 32
    inner_len = length // outer_len
    cos_outer, sin_outer, cos_twist, sin_twist, cos_inner, sin_inner = dft_tables(length)
    product = partial(jnp.einsum, precision=lax.Precision.HIGHEST)
    real_part = real_part.reshape(row_total, outer_len, inner_len)
    imag_part = imag_part.reshape(row_total, outer_len, inner_len)
    step_real = product("rab,ak->rkb", real_part, cos_outer) - product(
        "rab,ak->rkb", imag_part, sin_outer
    )
    step_imag = product("rab,ak->rkb", real_part, sin_outer) + product(
        "rab,ak->rkb", imag_part, cos_outer
    )
    twist_real = step_real * cos_twist - step_imag * sin_twist
    twist_imag = step_real * sin_twist + step_imag * cos_twist
    out_real = product("rkb,bm->rmk", twist_real, cos_inner) - product(
        "rkb,bm->rmk", twist_imag, sin_inner
    )
    out_imag = product("rkb,bm->rmk", twist_real, sin_inner) + product(
        "rkb,bm->rmk", twist_imag, cos_inner
    )
    return (out_real.reshape(row_total, length), out_imag.reshape(row_total, length))


def transform_first_real(real_part, imag_part):
    length, col_total = real_part.shape
    outer_len = 32
    inner_len = length // outer_len
    cos_outer, sin_outer, cos_twist, sin_twist, cos_inner, sin_inner = dft_tables(length)
    product = partial(jnp.einsum, precision=lax.Precision.HIGHEST)
    real_part = real_part.reshape(outer_len, inner_len, col_total)
    imag_part = imag_part.reshape(outer_len, inner_len, col_total)
    step_real = product("abc,ak->kbc", real_part, cos_outer) - product(
        "abc,ak->kbc", imag_part, sin_outer
    )
    step_imag = product("abc,ak->kbc", real_part, sin_outer) + product(
        "abc,ak->kbc", imag_part, cos_outer
    )
    twist_real = step_real * cos_twist[:, :, None] - step_imag * sin_twist[:, :, None]
    twist_imag = step_real * sin_twist[:, :, None] + step_imag * cos_twist[:, :, None]
    out_real = product("kbc,bm->mkc", twist_real, cos_inner) - product(
        "kbc,bm->mkc", twist_imag, sin_inner
    )
    return out_real.reshape(length, col_total)


PAY_ROWS = 19


GROUP = 8


def grid_kernel(order_ref, tile_ref, count_ref, pay_ref, out_ref):
    tiles_total = out_ref.shape[1] // TU * (out_ref.shape[2] // TV)
    tile_cols = out_ref.shape[2] // TV
    lanes = pay_ref.shape[2]
    out_ref[...] = jnp.zeros(out_ref.shape, jnp.float32)
    du_base = lax.broadcasted_iota(jnp.int32, (TU, lanes), 0)
    dv_base = lax.broadcasted_iota(jnp.int32, (TV, lanes), 0)

    def one_block(slot):
        blk = pay_ref[slot].astype(jnp.float32)
        vis = blk[0:2]
        ku = blk[2:9]
        kv = blk[9:16]
        ou = blk[16:17].astype(jnp.int32)
        ov = blk[17:18].astype(jnp.int32)
        du = du_base - ou
        su = jnp.zeros((TU, lanes), jnp.float32)
        for t in range(7):
            su = jnp.where(du == t, ku[t : t + 1], su)
        left = jnp.concatenate([vis[0:1] * su, vis[1:2] * su], axis=0).astype(jnp.bfloat16)
        dv = dv_base - ov
        sv = jnp.zeros((TV, lanes), jnp.float32)
        for t in range(7):
            sv = jnp.where(dv == t, kv[t : t + 1], sv)
        sv = sv.astype(jnp.bfloat16)
        return lax.dot_general(
            left, sv, (((1,), (1,)), ((), ())), preferred_element_type=jnp.float32
        )

    def body(i, carry):
        slots = [order_ref[i * GROUP + g] for g in range(GROUP)]
        contribs = [one_block(s) for s in slots]
        for s, contrib in zip(slots, contribs):
            tile = jnp.minimum(tile_ref[s], tiles_total - 1)
            row0 = pl.multiple_of((tile // tile_cols) * TU, TU)
            col0 = pl.multiple_of((tile % tile_cols) * TV, TV)

            @pl.when(tile_ref[s] < tiles_total)
            def _():
                for p in range(2):
                    out_ref[p, pl.ds(row0, TU), pl.ds(col0, TV)] += contrib[
                        p * TU : (p + 1) * TU
                    ]
        return carry

    steps = (count_ref[0] + GROUP - 1) // GROUP
    lax.fori_loop(0, steps, body, 0)


def grid_into_slab(order, tile_ids, count, payload, slab_rows):
    return pl.pallas_call(
        grid_kernel,
        out_shape=jax.ShapeDtypeStruct((2, slab_rows, GRID), jnp.float32),
        in_specs=[
            pl.BlockSpec(memory_space=pltpu.SMEM),
            pl.BlockSpec(memory_space=pltpu.SMEM),
            pl.BlockSpec(memory_space=pltpu.SMEM),
            pl.BlockSpec(memory_space=pltpu.VMEM),
        ],
        out_specs=pl.BlockSpec(memory_space=pltpu.VMEM),
    )(order, tile_ids, count, payload)


def shards(
    vis_values, kernel_u, kernel_v, offset_u, offset_v, block_owner, tile_slot, channel_freq
):
    row_count = lax.axis_size("row")
    block_count = vis_values.shape[1]
    vis_count = vis_values.shape[3]
    capacity = max(2, 4 * block_count // row_count)
    slot_count = row_count * capacity
    slab_rows = GRID // row_count
    tiles_total = slab_rows // TU * (GRID // TV)
    owner_row = block_owner[0, :, 0]
    row_marks = (owner_row[:, None] == jnp.arange(row_count, dtype=jnp.int32)[None, :]).astype(
        jnp.int32
    )
    before = jnp.cumsum(row_marks, axis=0) - row_marks
    slot_rank = jnp.sum(before * row_marks, axis=1)
    target = owner_row * capacity + slot_rank
    tile_row = jnp.broadcast_to(
        tile_slot[0][:, None, None].astype(jnp.bfloat16), (block_count, 1, vis_count)
    )
    payload = jnp.concatenate(
        [
            vis_values[0],
            kernel_u[0],
            kernel_v[0],
            offset_u[0][:, None, :].astype(jnp.bfloat16),
            offset_v[0][:, None, :].astype(jnp.bfloat16),
            tile_row,
        ],
        axis=1,
    )
    pick = (target[None, :] == jnp.arange(slot_count, dtype=jnp.int32)[:, None]).astype(
        jnp.bfloat16
    )
    send = jnp.einsum(
        "sb,bkn->skn", pick, payload, preferred_element_type=jnp.float32
    )
    empty = 1.0 - jnp.sum(pick.astype(jnp.float32), axis=1)
    send = send.at[:, PAY_ROWS - 1, :].add(empty[:, None] * tiles_total)
    send = send.astype(jnp.bfloat16)
    recv = lax.all_to_all(
        send.reshape((row_count, capacity) + payload.shape[1:]),
        "row",
        split_axis=0,
        concat_axis=0,
        tiled=True,
    ).reshape((slot_count,) + payload.shape[1:])
    tile_ids = jnp.max(recv[:, PAY_ROWS - 1, :].astype(jnp.float32), axis=1).astype(jnp.int32)
    filled = tile_ids < tiles_total
    filled_i = filled.astype(jnp.int32)
    count = jnp.sum(filled_i)
    place = jnp.where(
        filled, jnp.cumsum(filled_i) - 1, count + jnp.cumsum(1 - filled_i) - 1
    )
    order = jnp.zeros((slot_count,), jnp.int32).at[place].set(
        jnp.arange(slot_count, dtype=jnp.int32)
    )
    slab_grid = grid_into_slab(order, tile_ids, count.reshape(1), recv, slab_rows)
    spec_real, spec_imag = transform_last(slab_grid[0], slab_grid[1])
    halves = 2
    half_cols = GRID // row_count // halves
    spectrum = jnp.stack([spec_real, spec_imag]).reshape(
        2, slab_rows, row_count, halves, half_cols
    )
    image_scale = 1.0 / math.sqrt(block_count * row_count * vis_count)
    offset_freq = (channel_freq[0] - 1.284) / 0.428
    weights = jnp.stack([jnp.ones_like(offset_freq), offset_freq, offset_freq * offset_freq])
    pieces = []
    for h in range(halves):
        received = lax.all_to_all(
            for_sending(spectrum[:, :, :, h, :]), "row", split_axis=2, concat_axis=1, tiled=True
        )
        if h > 0:
            received = lax.optimization_barrier((gate, received))[1]
        received = received.astype(jnp.float32)
        real_cols = received[0].reshape(GRID, half_cols)
        imag_cols = received[1].reshape(GRID, half_cols)
        dirty_image = transform_first_real(real_cols, imag_cols) * image_scale
        taylor_terms = (weights[:, None, None] * dirty_image[None]).astype(jnp.bfloat16)
        pieces.append(
            lax.psum_scatter(taylor_terms, "freq", scatter_dimension=1, tiled=True)
        )
        gate = pieces[-1]
    summed = jnp.concatenate(pieces, axis=2)
    return summed


def solution(mesh):
    return jax.shard_map(
        shards,
        mesh=mesh,
        in_specs=(
            P("freq", "row", None, None),
            P("freq", "row", None, None),
            P("freq", "row", None, None),
            P("freq", "row", None),
            P("freq", "row", None),
            P("freq", "row", None),
            P("freq", "row"),
            P("freq"),
        ),
        out_specs=P(None, "freq", "row"),
        check_vma=False,
    )
```

```python
from functools import partial
import math

import jax
import jax.numpy as jnp
from jax import lax
from jax.sharding import Mesh, PartitionSpec as P
from jax.experimental import pallas as pl
from jax.experimental.pallas import tpu as pltpu

GRID = 4096
TU = 16
TV = 128


def for_sending(shard):
    return jax.tree.map(lambda a: a.astype(jnp.bfloat16) if a.dtype == jnp.float32 else a, shard)


def dft_tables(length):
    outer_len = 32
    inner_len = length // outer_len
    index_outer = jnp.arange(outer_len, dtype=jnp.int32)
    index_inner = jnp.arange(inner_len, dtype=jnp.int32)
    full_turn = 2.0 * math.pi
    angle_outer = (
        full_turn
        * (index_outer[:, None] * index_outer[None, :] % outer_len).astype(jnp.float32)
        / outer_len
    )
    angle_twist = (
        full_turn
        * (index_outer[:, None] * index_inner[None, :] % length).astype(jnp.float32)
        / length
    )
    angle_inner = (
        full_turn
        * (index_inner[:, None] * index_inner[None, :] % inner_len).astype(jnp.float32)
        / inner_len
    )
    return (
        jnp.cos(angle_outer),
        jnp.sin(angle_outer),
        jnp.cos(angle_twist),
        jnp.sin(angle_twist),
        jnp.cos(angle_inner),
        jnp.sin(angle_inner),
    )


def transform_last(real_part, imag_part):
    row_total, length = real_part.shape
    outer_len = 32
    inner_len = length // outer_len
    cos_outer, sin_outer, cos_twist, sin_twist, cos_inner, sin_inner = dft_tables(length)
    product = partial(jnp.einsum, precision=lax.Precision.HIGHEST)
    real_part = real_part.reshape(row_total, outer_len, inner_len)
    imag_part = imag_part.reshape(row_total, outer_len, inner_len)
    step_real = product("rab,ak->rkb", real_part, cos_outer) - product(
        "rab,ak->rkb", imag_part, sin_outer
    )
    step_imag = product("rab,ak->rkb", real_part, sin_outer) + product(
        "rab,ak->rkb", imag_part, cos_outer
    )
    twist_real = step_real * cos_twist - step_imag * sin_twist
    twist_imag = step_real * sin_twist + step_imag * cos_twist
    out_real = product("rkb,bm->rmk", twist_real, cos_inner) - product(
        "rkb,bm->rmk", twist_imag, sin_inner
    )
    out_imag = product("rkb,bm->rmk", twist_real, sin_inner) + product(
        "rkb,bm->rmk", twist_imag, cos_inner
    )
    return (out_real.reshape(row_total, length), out_imag.reshape(row_total, length))


def transform_first_real(real_part, imag_part):
    length, col_total = real_part.shape
    outer_len = 32
    inner_len = length // outer_len
    cos_outer, sin_outer, cos_twist, sin_twist, cos_inner, sin_inner = dft_tables(length)
    product = partial(jnp.einsum, precision=lax.Precision.HIGHEST)
    real_part = real_part.reshape(outer_len, inner_len, col_total)
    imag_part = imag_part.reshape(outer_len, inner_len, col_total)
    step_real = product("abc,ak->kbc", real_part, cos_outer) - product(
        "abc,ak->kbc", imag_part, sin_outer
    )
    step_imag = product("abc,ak->kbc", real_part, sin_outer) + product(
        "abc,ak->kbc", imag_part, cos_outer
    )
    twist_real = step_real * cos_twist[:, :, None] - step_imag * sin_twist[:, :, None]
    twist_imag = step_real * sin_twist[:, :, None] + step_imag * cos_twist[:, :, None]
    out_real = product("kbc,bm->mkc", twist_real, cos_inner) - product(
        "kbc,bm->mkc", twist_imag, sin_inner
    )
    return out_real.reshape(length, col_total)


PAY_ROWS = 19


GROUP = 8


def grid_kernel(order_ref, tile_ref, count_ref, pay_ref, out_ref):
    tiles_total = out_ref.shape[1] // TU * (out_ref.shape[2] // TV)
    tile_cols = out_ref.shape[2] // TV
    lanes = pay_ref.shape[2]
    out_ref[...] = jnp.zeros(out_ref.shape, jnp.float32)
    du_base = lax.broadcasted_iota(jnp.int32, (TU, lanes), 0)
    dv_base = lax.broadcasted_iota(jnp.int32, (TV, lanes), 0)

    def one_block(slot):
        blk = pay_ref[slot].astype(jnp.float32)
        vis = blk[0:2]
        ku = blk[2:9]
        kv = blk[9:16]
        ou = blk[16:17].astype(jnp.int32)
        ov = blk[17:18].astype(jnp.int32)
        du = du_base - ou
        su = jnp.zeros((TU, lanes), jnp.float32)
        for t in range(7):
            su = jnp.where(du == t, ku[t : t + 1], su)
        left = jnp.concatenate([vis[0:1] * su, vis[1:2] * su], axis=0).astype(jnp.bfloat16)
        dv = dv_base - ov
        sv = jnp.zeros((TV, lanes), jnp.float32)
        for t in range(7):
            sv = jnp.where(dv == t, kv[t : t + 1], sv)
        sv = sv.astype(jnp.bfloat16)
        return lax.dot_general(
            left, sv, (((1,), (1,)), ((), ())), preferred_element_type=jnp.float32
        )

    def body(i, carry):
        slots = [order_ref[i * GROUP + g] for g in range(GROUP)]
        contribs = [one_block(s) for s in slots]
        for s, contrib in zip(slots, contribs):
            tile = jnp.minimum(tile_ref[s], tiles_total - 1)
            row0 = pl.multiple_of((tile // tile_cols) * TU, TU)
            col0 = pl.multiple_of((tile % tile_cols) * TV, TV)

            @pl.when(tile_ref[s] < tiles_total)
            def _():
                for p in range(2):
                    out_ref[p, pl.ds(row0, TU), pl.ds(col0, TV)] += contrib[
                        p * TU : (p + 1) * TU
                    ]
        return carry

    steps = (count_ref[0] + GROUP - 1) // GROUP
    lax.fori_loop(0, steps, body, 0)


def grid_into_slab(order, tile_ids, count, payload, slab_rows):
    return pl.pallas_call(
        grid_kernel,
        out_shape=jax.ShapeDtypeStruct((2, slab_rows, GRID), jnp.float32),
        in_specs=[
            pl.BlockSpec(memory_space=pltpu.SMEM),
            pl.BlockSpec(memory_space=pltpu.SMEM),
            pl.BlockSpec(memory_space=pltpu.SMEM),
            pl.BlockSpec(memory_space=pltpu.VMEM),
        ],
        out_specs=pl.BlockSpec(memory_space=pltpu.VMEM),
    )(order, tile_ids, count, payload)


def shards(
    vis_values, kernel_u, kernel_v, offset_u, offset_v, block_owner, tile_slot, channel_freq
):
    row_count = lax.axis_size("row")
    block_count = vis_values.shape[1]
    vis_count = vis_values.shape[3]
    capacity = max(2, 4 * block_count // row_count)
    slot_count = row_count * capacity
    slab_rows = GRID // row_count
    tiles_total = slab_rows // TU * (GRID // TV)
    owner_row = block_owner[0, :, 0]
    row_marks = (owner_row[:, None] == jnp.arange(row_count, dtype=jnp.int32)[None, :]).astype(
        jnp.int32
    )
    before = jnp.cumsum(row_marks, axis=0) - row_marks
    slot_rank = jnp.sum(before * row_marks, axis=1)
    target = owner_row * capacity + slot_rank
    tile_row = jnp.broadcast_to(
        tile_slot[0][:, None, None].astype(jnp.bfloat16), (block_count, 1, vis_count)
    )
    payload = jnp.concatenate(
        [
            vis_values[0],
            kernel_u[0],
            kernel_v[0],
            offset_u[0][:, None, :].astype(jnp.bfloat16),
            offset_v[0][:, None, :].astype(jnp.bfloat16),
            tile_row,
        ],
        axis=1,
    )
    pick = (target[None, :] == jnp.arange(slot_count, dtype=jnp.int32)[:, None]).astype(
        jnp.bfloat16
    )
    send = jnp.einsum(
        "sb,bkn->skn", pick, payload, preferred_element_type=jnp.float32
    )
    empty = 1.0 - jnp.sum(pick.astype(jnp.float32), axis=1)
    send = send.at[:, PAY_ROWS - 1, :].add(empty[:, None] * tiles_total)
    send = send.astype(jnp.bfloat16)
    recv = lax.all_to_all(
        send.reshape((row_count, capacity) + payload.shape[1:]),
        "row",
        split_axis=0,
        concat_axis=0,
        tiled=True,
    ).reshape((slot_count,) + payload.shape[1:])
    tile_ids = jnp.max(recv[:, PAY_ROWS - 1, :].astype(jnp.float32), axis=1).astype(jnp.int32)
    filled = tile_ids < tiles_total
    filled_i = filled.astype(jnp.int32)
    count = jnp.sum(filled_i)
    place = jnp.where(
        filled, jnp.cumsum(filled_i) - 1, count + jnp.cumsum(1 - filled_i) - 1
    )
    order = jnp.zeros((slot_count,), jnp.int32).at[place].set(
        jnp.arange(slot_count, dtype=jnp.int32)
    )
    slab_grid = grid_into_slab(order, tile_ids, count.reshape(1), recv, slab_rows)
    spec_real, spec_imag = transform_last(slab_grid[0], slab_grid[1])
    spectrum = jnp.stack([spec_real, spec_imag]).reshape(2, slab_rows, row_count, GRID // row_count)
    image_scale = 1.0 / math.sqrt(block_count * row_count * vis_count)
    offset_freq = (channel_freq[0] - 1.284) / 0.428
    weights = jnp.stack([jnp.ones_like(offset_freq), offset_freq, offset_freq * offset_freq])
    received = lax.all_to_all(
        for_sending(spectrum), "row", split_axis=2, concat_axis=1, tiled=True
    ).astype(spectrum.dtype)
    width_here = received.shape[2] * received.shape[3]
    real_cols = received[0].reshape(GRID, width_here)
    imag_cols = received[1].reshape(GRID, width_here)
    dirty_image = transform_first_real(real_cols, imag_cols) * image_scale
    taylor_terms = (weights[:, None, None] * dirty_image[None]).astype(jnp.bfloat16)
    chips = lax.axis_size("z")
    pair = lax.axis_size("core")
    core = lax.axis_index("core")
    terms = taylor_terms.astype(jnp.float32).reshape(3, chips, pair, GRID // chips // pair, width_here)
    keep = lax.dynamic_index_in_dim(terms, core, axis=2, keepdims=False)
    give = lax.dynamic_index_in_dim(terms, pair - 1 - core, axis=2, keepdims=False)
    got = lax.ppermute(give, "core", [(0, 1), (1, 0)])
    partial_sum = (keep + got).astype(jnp.bfloat16)
    summed = lax.psum_scatter(partial_sum, "z", scatter_dimension=1, tiled=True)
    summed = summed.reshape(3, GRID // chips // pair, width_here)
    return summed


def solution(mesh):
    chips = mesh.shape["freq"] // 2
    split = Mesh(mesh.devices.reshape(chips, 2, mesh.shape["row"]), ("z", "core", "row"))
    freq = ("z", "core")
    return jax.shard_map(
        shards,
        mesh=split,
        in_specs=(
            P(freq, "row", None, None),
            P(freq, "row", None, None),
            P(freq, "row", None, None),
            P(freq, "row", None),
            P(freq, "row", None),
            P(freq, "row", None),
            P(freq, "row"),
            P(freq),
        ),
        out_specs=P(None, freq, "row"),
        check_vma=False,
    )
```

```python
from functools import partial
import math

import jax
import jax.numpy as jnp
from jax import lax
from jax.sharding import Mesh, PartitionSpec as P
from jax.experimental import pallas as pl
from jax.experimental.pallas import tpu as pltpu

GRID = 4096
TU = 16
TV = 128


def for_sending(shard):
    return jax.tree.map(lambda a: a.astype(jnp.bfloat16) if a.dtype == jnp.float32 else a, shard)


def dft_tables(length):
    outer_len = 32
    inner_len = length // outer_len
    index_outer = jnp.arange(outer_len, dtype=jnp.int32)
    index_inner = jnp.arange(inner_len, dtype=jnp.int32)
    full_turn = 2.0 * math.pi
    angle_outer = (
        full_turn
        * (index_outer[:, None] * index_outer[None, :] % outer_len).astype(jnp.float32)
        / outer_len
    )
    angle_twist = (
        full_turn
        * (index_outer[:, None] * index_inner[None, :] % length).astype(jnp.float32)
        / length
    )
    angle_inner = (
        full_turn
        * (index_inner[:, None] * index_inner[None, :] % inner_len).astype(jnp.float32)
        / inner_len
    )
    return (
        jnp.cos(angle_outer),
        jnp.sin(angle_outer),
        jnp.cos(angle_twist),
        jnp.sin(angle_twist),
        jnp.cos(angle_inner),
        jnp.sin(angle_inner),
    )


def transform_last(real_part, imag_part):
    row_total, length = real_part.shape
    outer_len = 32
    inner_len = length // outer_len
    cos_outer, sin_outer, cos_twist, sin_twist, cos_inner, sin_inner = dft_tables(length)
    product = partial(jnp.einsum, precision=lax.Precision.HIGH)
    real_part = real_part.reshape(row_total, outer_len, inner_len)
    imag_part = imag_part.reshape(row_total, outer_len, inner_len)
    step_real = product("rab,ak->rkb", real_part, cos_outer) - product(
        "rab,ak->rkb", imag_part, sin_outer
    )
    step_imag = product("rab,ak->rkb", real_part, sin_outer) + product(
        "rab,ak->rkb", imag_part, cos_outer
    )
    twist_real = step_real * cos_twist - step_imag * sin_twist
    twist_imag = step_real * sin_twist + step_imag * cos_twist
    out_real = product("rkb,bm->rmk", twist_real, cos_inner) - product(
        "rkb,bm->rmk", twist_imag, sin_inner
    )
    out_imag = product("rkb,bm->rmk", twist_real, sin_inner) + product(
        "rkb,bm->rmk", twist_imag, cos_inner
    )
    return (out_real.reshape(row_total, length), out_imag.reshape(row_total, length))


def transform_first_real(real_part, imag_part):
    length, col_total = real_part.shape
    outer_len = 32
    inner_len = length // outer_len
    cos_outer, sin_outer, cos_twist, sin_twist, cos_inner, sin_inner = dft_tables(length)
    product = partial(jnp.einsum, precision=lax.Precision.HIGH)
    real_part = real_part.reshape(outer_len, inner_len, col_total)
    imag_part = imag_part.reshape(outer_len, inner_len, col_total)
    step_real = product("abc,ak->kbc", real_part, cos_outer) - product(
        "abc,ak->kbc", imag_part, sin_outer
    )
    step_imag = product("abc,ak->kbc", real_part, sin_outer) + product(
        "abc,ak->kbc", imag_part, cos_outer
    )
    twist_real = step_real * cos_twist[:, :, None] - step_imag * sin_twist[:, :, None]
    twist_imag = step_real * sin_twist[:, :, None] + step_imag * cos_twist[:, :, None]
    out_real = product("kbc,bm->mkc", twist_real, cos_inner) - product(
        "kbc,bm->mkc", twist_imag, sin_inner
    )
    return out_real.reshape(length, col_total)


PAY_ROWS = 19


GROUP = 8


def grid_kernel(order_ref, tile_ref, count_ref, pay_ref, out_ref):
    tiles_total = out_ref.shape[1] // TU * (out_ref.shape[2] // TV)
    tile_cols = out_ref.shape[2] // TV
    lanes = pay_ref.shape[2]
    out_ref[...] = jnp.zeros(out_ref.shape, jnp.float32)
    du_base = lax.broadcasted_iota(jnp.int32, (TU, lanes), 0)
    dv_base = lax.broadcasted_iota(jnp.int32, (TV, lanes), 0)

    def one_block(slot):
        blk = pay_ref[slot].astype(jnp.float32)
        vis = blk[0:2]
        ku = blk[2:9]
        kv = blk[9:16]
        ou = blk[16:17].astype(jnp.int32)
        ov = blk[17:18].astype(jnp.int32)
        du = du_base - ou
        su = jnp.zeros((TU, lanes), jnp.float32)
        for t in range(7):
            su = jnp.where(du == t, ku[t : t + 1], su)
        left = jnp.concatenate([vis[0:1] * su, vis[1:2] * su], axis=0).astype(jnp.bfloat16)
        dv = dv_base - ov
        sv = jnp.zeros((TV, lanes), jnp.float32)
        for t in range(7):
            sv = jnp.where(dv == t, kv[t : t + 1], sv)
        sv = sv.astype(jnp.bfloat16)
        return lax.dot_general(
            left, sv, (((1,), (1,)), ((), ())), preferred_element_type=jnp.float32
        )

    def body(i, carry):
        slots = [order_ref[i * GROUP + g] for g in range(GROUP)]
        contribs = [one_block(s) for s in slots]
        for s, contrib in zip(slots, contribs):
            tile = jnp.minimum(tile_ref[s], tiles_total - 1)
            row0 = pl.multiple_of((tile // tile_cols) * TU, TU)
            col0 = pl.multiple_of((tile % tile_cols) * TV, TV)

            @pl.when(tile_ref[s] < tiles_total)
            def _():
                for p in range(2):
                    out_ref[p, pl.ds(row0, TU), pl.ds(col0, TV)] += contrib[
                        p * TU : (p + 1) * TU
                    ]
        return carry

    steps = (count_ref[0] + GROUP - 1) // GROUP
    lax.fori_loop(0, steps, body, 0)


def grid_into_slab(order, tile_ids, count, payload, slab_rows):
    return pl.pallas_call(
        grid_kernel,
        out_shape=jax.ShapeDtypeStruct((2, slab_rows, GRID), jnp.float32),
        in_specs=[
            pl.BlockSpec(memory_space=pltpu.SMEM),
            pl.BlockSpec(memory_space=pltpu.SMEM),
            pl.BlockSpec(memory_space=pltpu.SMEM),
            pl.BlockSpec(memory_space=pltpu.VMEM),
        ],
        out_specs=pl.BlockSpec(memory_space=pltpu.VMEM),
    )(order, tile_ids, count, payload)


def shards(
    vis_values, kernel_u, kernel_v, offset_u, offset_v, block_owner, tile_slot, channel_freq
):
    row_count = lax.axis_size("row")
    block_count = vis_values.shape[1]
    vis_count = vis_values.shape[3]
    capacity = max(2, 4 * block_count // row_count)
    slot_count = row_count * capacity
    slab_rows = GRID // row_count
    tiles_total = slab_rows // TU * (GRID // TV)
    owner_row = block_owner[0, :, 0]
    row_marks = (owner_row[:, None] == jnp.arange(row_count, dtype=jnp.int32)[None, :]).astype(
        jnp.int32
    )
    before = jnp.cumsum(row_marks, axis=0) - row_marks
    slot_rank = jnp.sum(before * row_marks, axis=1)
    target = owner_row * capacity + slot_rank
    tile_row = jnp.broadcast_to(
        tile_slot[0][:, None, None].astype(jnp.bfloat16), (block_count, 1, vis_count)
    )
    payload = jnp.concatenate(
        [
            vis_values[0],
            kernel_u[0],
            kernel_v[0],
            offset_u[0][:, None, :].astype(jnp.bfloat16),
            offset_v[0][:, None, :].astype(jnp.bfloat16),
            tile_row,
        ],
        axis=1,
    )
    pick = (target[None, :] == jnp.arange(slot_count, dtype=jnp.int32)[:, None]).astype(
        jnp.bfloat16
    )
    send = jnp.einsum(
        "sb,bkn->skn", pick, payload, preferred_element_type=jnp.float32
    )
    empty = 1.0 - jnp.sum(pick.astype(jnp.float32), axis=1)
    send = send.at[:, PAY_ROWS - 1, :].add(empty[:, None] * tiles_total)
    send = send.astype(jnp.bfloat16)
    recv = lax.all_to_all(
        send.reshape((row_count, capacity) + payload.shape[1:]),
        "row",
        split_axis=0,
        concat_axis=0,
        tiled=True,
    ).reshape((slot_count,) + payload.shape[1:])
    tile_ids = jnp.max(recv[:, PAY_ROWS - 1, :].astype(jnp.float32), axis=1).astype(jnp.int32)
    filled = tile_ids < tiles_total
    filled_i = filled.astype(jnp.int32)
    count = jnp.sum(filled_i)
    place = jnp.where(
        filled, jnp.cumsum(filled_i) - 1, count + jnp.cumsum(1 - filled_i) - 1
    )
    order = jnp.zeros((slot_count,), jnp.int32).at[place].set(
        jnp.arange(slot_count, dtype=jnp.int32)
    )
    slab_grid = grid_into_slab(order, tile_ids, count.reshape(1), recv, slab_rows)
    spec_real, spec_imag = transform_last(slab_grid[0], slab_grid[1])
    spectrum = jnp.stack([spec_real, spec_imag]).reshape(2, slab_rows, row_count, GRID // row_count)
    image_scale = 1.0 / math.sqrt(block_count * row_count * vis_count)
    offset_freq = (channel_freq[0] - 1.284) / 0.428
    weights = jnp.stack([jnp.ones_like(offset_freq), offset_freq, offset_freq * offset_freq])
    received = lax.all_to_all(
        for_sending(spectrum), "row", split_axis=2, concat_axis=1, tiled=True
    ).astype(spectrum.dtype)
    width_here = received.shape[2] * received.shape[3]
    real_cols = received[0].reshape(GRID, width_here)
    imag_cols = received[1].reshape(GRID, width_here)
    dirty_image = transform_first_real(real_cols, imag_cols) * image_scale
    taylor_terms = (weights[:, None, None] * dirty_image[None]).astype(jnp.bfloat16)
    chips = lax.axis_size("z")
    pair = lax.axis_size("core")
    core = lax.axis_index("core")
    terms = taylor_terms.reshape(3, chips, pair, GRID // chips // pair, width_here)
    keep = lax.dynamic_index_in_dim(terms, core, axis=2, keepdims=False)
    give = lax.dynamic_index_in_dim(terms, pair - 1 - core, axis=2, keepdims=False)
    got = lax.ppermute(give, "core", [(0, 1), (1, 0)])
    partial_sum = (keep.astype(jnp.float32) + got.astype(jnp.float32)).astype(jnp.bfloat16)
    summed = lax.psum_scatter(partial_sum, "z", scatter_dimension=1, tiled=True)
    summed = summed.reshape(3, GRID // chips // pair, width_here)
    return summed


def solution(mesh):
    chips = mesh.shape["freq"] // 2
    split = Mesh(mesh.devices.reshape(chips, 2, mesh.shape["row"]), ("z", "core", "row"))
    freq = ("z", "core")
    return jax.shard_map(
        shards,
        mesh=split,
        in_specs=(
            P(freq, "row", None, None),
            P(freq, "row", None, None),
            P(freq, "row", None, None),
            P(freq, "row", None),
            P(freq, "row", None),
            P(freq, "row", None),
            P(freq, "row"),
            P(freq),
        ),
        out_specs=P(None, freq, "row"),
        check_vma=False,
    )
```

```python
from functools import partial
import math

import jax
import jax.numpy as jnp
from jax import lax
from jax.sharding import Mesh, PartitionSpec as P
from jax.experimental import pallas as pl
from jax.experimental.pallas import tpu as pltpu

GRID = 4096
TU = 16
TV = 128


def for_sending(shard):
    return jax.tree.map(lambda a: a.astype(jnp.bfloat16) if a.dtype == jnp.float32 else a, shard)


def dft_tables(length):
    outer_len = 32
    inner_len = length // outer_len
    index_outer = jnp.arange(outer_len, dtype=jnp.int32)
    index_inner = jnp.arange(inner_len, dtype=jnp.int32)
    full_turn = 2.0 * math.pi
    angle_outer = (
        full_turn
        * (index_outer[:, None] * index_outer[None, :] % outer_len).astype(jnp.float32)
        / outer_len
    )
    angle_twist = (
        full_turn
        * (index_outer[:, None] * index_inner[None, :] % length).astype(jnp.float32)
        / length
    )
    angle_inner = (
        full_turn
        * (index_inner[:, None] * index_inner[None, :] % inner_len).astype(jnp.float32)
        / inner_len
    )
    return (
        jnp.cos(angle_outer),
        jnp.sin(angle_outer),
        jnp.cos(angle_twist),
        jnp.sin(angle_twist),
        jnp.cos(angle_inner),
        jnp.sin(angle_inner),
    )


def complex_weights(cos_part, sin_part, real_only=False):
    top = jnp.concatenate([cos_part, sin_part], axis=1)
    bottom = jnp.concatenate([-sin_part, cos_part], axis=1)
    if real_only:
        return jnp.stack([cos_part, -sin_part])
    return jnp.stack([top, bottom])


def transform_last(real_part, imag_part):
    row_total, length = real_part.shape
    outer_len = 32
    inner_len = length // outer_len
    cos_outer, sin_outer, cos_twist, sin_twist, cos_inner, sin_inner = dft_tables(length)
    product = partial(jnp.einsum, precision=lax.Precision.HIGH)
    both = jnp.stack([real_part, imag_part]).reshape(2, row_total, outer_len, inner_len)
    step = product("prab,pak->rkb", both, complex_weights(cos_outer, sin_outer))
    step_real = step[:, :outer_len]
    step_imag = step[:, outer_len:]
    twist_real = step_real * cos_twist - step_imag * sin_twist
    twist_imag = step_real * sin_twist + step_imag * cos_twist
    out = product(
        "qrkb,qbm->rmk",
        jnp.stack([twist_real, twist_imag]),
        complex_weights(cos_inner, sin_inner),
    )
    out_real = out[:, :inner_len].reshape(row_total, length)
    out_imag = out[:, inner_len:].reshape(row_total, length)
    return (out_real, out_imag)


def transform_first_real(both):
    _, length, col_total = both.shape
    outer_len = 32
    inner_len = length // outer_len
    cos_outer, sin_outer, cos_twist, sin_twist, cos_inner, sin_inner = dft_tables(length)
    product = partial(jnp.einsum, precision=lax.Precision.HIGH)
    both = both.reshape(2, outer_len, inner_len, col_total)
    step = product("pabc,pak->kbc", both, complex_weights(cos_outer, sin_outer))
    step_real = step[:outer_len]
    step_imag = step[outer_len:]
    twist_real = step_real * cos_twist[:, :, None] - step_imag * sin_twist[:, :, None]
    twist_imag = step_real * sin_twist[:, :, None] + step_imag * cos_twist[:, :, None]
    out_real = product(
        "qkbc,qbm->mkc",
        jnp.stack([twist_real, twist_imag]),
        complex_weights(cos_inner, sin_inner, real_only=True),
    )
    return out_real.reshape(length, col_total)


PAY_ROWS = 19


GROUP = 8


def grid_kernel(order_ref, tile_ref, count_ref, pay_ref, out_ref):
    tiles_total = out_ref.shape[1] // TU * (out_ref.shape[2] // TV)
    tile_cols = out_ref.shape[2] // TV
    lanes = pay_ref.shape[2]
    out_ref[...] = jnp.zeros(out_ref.shape, jnp.float32)
    du_base = lax.broadcasted_iota(jnp.int32, (TU, lanes), 0)
    dv_base = lax.broadcasted_iota(jnp.int32, (TV, lanes), 0)

    def one_block(slot):
        blk = pay_ref[slot].astype(jnp.float32)
        vis = blk[0:2]
        ku = blk[2:9]
        kv = blk[9:16]
        ou = blk[16:17].astype(jnp.int32)
        ov = blk[17:18].astype(jnp.int32)
        du = du_base - ou
        su = jnp.zeros((TU, lanes), jnp.float32)
        for t in range(7):
            su = jnp.where(du == t, ku[t : t + 1], su)
        left = jnp.concatenate([vis[0:1] * su, vis[1:2] * su], axis=0).astype(jnp.bfloat16)
        dv = dv_base - ov
        sv = jnp.zeros((TV, lanes), jnp.float32)
        for t in range(7):
            sv = jnp.where(dv == t, kv[t : t + 1], sv)
        sv = sv.astype(jnp.bfloat16)
        return lax.dot_general(
            left, sv, (((1,), (1,)), ((), ())), preferred_element_type=jnp.float32
        )

    def body(i, carry):
        slots = [order_ref[i * GROUP + g] for g in range(GROUP)]
        contribs = [one_block(s) for s in slots]
        for s, contrib in zip(slots, contribs):
            tile = jnp.minimum(tile_ref[s], tiles_total - 1)
            row0 = pl.multiple_of((tile // tile_cols) * TU, TU)
            col0 = pl.multiple_of((tile % tile_cols) * TV, TV)

            @pl.when(tile_ref[s] < tiles_total)
            def _():
                for p in range(2):
                    out_ref[p, pl.ds(row0, TU), pl.ds(col0, TV)] += contrib[
                        p * TU : (p + 1) * TU
                    ]
        return carry

    steps = (count_ref[0] + GROUP - 1) // GROUP
    lax.fori_loop(0, steps, body, 0)


def grid_into_slab(order, tile_ids, count, payload, slab_rows):
    return pl.pallas_call(
        grid_kernel,
        out_shape=jax.ShapeDtypeStruct((2, slab_rows, GRID), jnp.float32),
        in_specs=[
            pl.BlockSpec(memory_space=pltpu.SMEM),
            pl.BlockSpec(memory_space=pltpu.SMEM),
            pl.BlockSpec(memory_space=pltpu.SMEM),
            pl.BlockSpec(memory_space=pltpu.VMEM),
        ],
        out_specs=pl.BlockSpec(memory_space=pltpu.VMEM),
    )(order, tile_ids, count, payload)


def shards(
    vis_values, kernel_u, kernel_v, offset_u, offset_v, block_owner, tile_slot, channel_freq
):
    row_count = lax.axis_size("row")
    block_count = vis_values.shape[1]
    vis_count = vis_values.shape[3]
    capacity = max(2, 4 * block_count // row_count)
    slot_count = row_count * capacity
    slab_rows = GRID // row_count
    tiles_total = slab_rows // TU * (GRID // TV)
    owner_row = block_owner[0, :, 0]
    row_marks = (owner_row[:, None] == jnp.arange(row_count, dtype=jnp.int32)[None, :]).astype(
        jnp.int32
    )
    before = jnp.cumsum(row_marks, axis=0) - row_marks
    slot_rank = jnp.sum(before * row_marks, axis=1)
    target = owner_row * capacity + slot_rank
    tile_row = jnp.broadcast_to(
        tile_slot[0][:, None, None].astype(jnp.bfloat16), (block_count, 1, vis_count)
    )
    payload = jnp.concatenate(
        [
            vis_values[0],
            kernel_u[0],
            kernel_v[0],
            offset_u[0][:, None, :].astype(jnp.bfloat16),
            offset_v[0][:, None, :].astype(jnp.bfloat16),
            tile_row,
        ],
        axis=1,
    )
    pick = (target[None, :] == jnp.arange(slot_count, dtype=jnp.int32)[:, None]).astype(
        jnp.bfloat16
    )
    send = jnp.einsum(
        "sb,bkn->skn", pick, payload, preferred_element_type=jnp.float32
    )
    empty = 1.0 - jnp.sum(pick.astype(jnp.float32), axis=1)
    send = send.at[:, PAY_ROWS - 1, :].add(empty[:, None] * tiles_total)
    send = send.astype(jnp.bfloat16)
    recv = lax.all_to_all(
        send.reshape((row_count, capacity) + payload.shape[1:]),
        "row",
        split_axis=0,
        concat_axis=0,
        tiled=True,
    ).reshape((slot_count,) + payload.shape[1:])
    tile_ids = jnp.max(recv[:, PAY_ROWS - 1, :].astype(jnp.float32), axis=1).astype(jnp.int32)
    filled = tile_ids < tiles_total
    filled_i = filled.astype(jnp.int32)
    count = jnp.sum(filled_i)
    place = jnp.where(
        filled, jnp.cumsum(filled_i) - 1, count + jnp.cumsum(1 - filled_i) - 1
    )
    order = jnp.zeros((slot_count,), jnp.int32).at[place].set(
        jnp.arange(slot_count, dtype=jnp.int32)
    )
    slab_grid = grid_into_slab(order, tile_ids, count.reshape(1), recv, slab_rows)
    spec_real, spec_imag = transform_last(slab_grid[0], slab_grid[1])
    spectrum = jnp.stack([spec_real, spec_imag]).reshape(2, slab_rows, row_count, GRID // row_count)
    image_scale = 1.0 / math.sqrt(block_count * row_count * vis_count)
    offset_freq = (channel_freq[0] - 1.284) / 0.428
    weights = jnp.stack([jnp.ones_like(offset_freq), offset_freq, offset_freq * offset_freq])
    received = lax.all_to_all(
        for_sending(spectrum), "row", split_axis=2, concat_axis=1, tiled=True
    ).astype(spectrum.dtype)
    width_here = received.shape[2] * received.shape[3]
    dirty_image = transform_first_real(received.reshape(2, GRID, width_here)) * image_scale
    taylor_terms = (weights[:, None, None] * dirty_image[None]).astype(jnp.bfloat16)
    chips = lax.axis_size("z")
    pair = lax.axis_size("core")
    core = lax.axis_index("core")
    terms = taylor_terms.reshape(3, chips, pair, GRID // chips // pair, width_here)
    keep = lax.dynamic_index_in_dim(terms, core, axis=2, keepdims=False)
    give = lax.dynamic_index_in_dim(terms, pair - 1 - core, axis=2, keepdims=False)
    got = lax.ppermute(give, "core", [(0, 1), (1, 0)])
    partial_sum = (keep.astype(jnp.float32) + got.astype(jnp.float32)).astype(jnp.bfloat16)
    summed = lax.psum_scatter(partial_sum, "z", scatter_dimension=1, tiled=True)
    summed = summed.reshape(3, GRID // chips // pair, width_here)
    return summed


def solution(mesh):
    chips = mesh.shape["freq"] // 2
    split = Mesh(mesh.devices.reshape(chips, 2, mesh.shape["row"]), ("z", "core", "row"))
    freq = ("z", "core")
    return jax.shard_map(
        shards,
        mesh=split,
        in_specs=(
            P(freq, "row", None, None),
            P(freq, "row", None, None),
            P(freq, "row", None, None),
            P(freq, "row", None),
            P(freq, "row", None),
            P(freq, "row", None),
            P(freq, "row"),
            P(freq),
        ),
        out_specs=P(None, freq, "row"),
        check_vma=False,
    )
```

```python
from functools import partial
import math

import jax
import jax.numpy as jnp
from jax import lax
from jax.sharding import Mesh, PartitionSpec as P
from jax.experimental import pallas as pl
from jax.experimental.pallas import tpu as pltpu

GRID = 4096
TU = 16
TV = 128


def for_sending(shard):
    return jax.tree.map(lambda a: a.astype(jnp.bfloat16) if a.dtype == jnp.float32 else a, shard)


def dft_tables(length):
    outer_len = 32
    inner_len = length // outer_len
    index_outer = jnp.arange(outer_len, dtype=jnp.int32)
    index_inner = jnp.arange(inner_len, dtype=jnp.int32)
    full_turn = 2.0 * math.pi
    angle_outer = (
        full_turn
        * (index_outer[:, None] * index_outer[None, :] % outer_len).astype(jnp.float32)
        / outer_len
    )
    angle_twist = (
        full_turn
        * (index_outer[:, None] * index_inner[None, :] % length).astype(jnp.float32)
        / length
    )
    angle_inner = (
        full_turn
        * (index_inner[:, None] * index_inner[None, :] % inner_len).astype(jnp.float32)
        / inner_len
    )
    return (
        jnp.cos(angle_outer),
        jnp.sin(angle_outer),
        jnp.cos(angle_twist),
        jnp.sin(angle_twist),
        jnp.cos(angle_inner),
        jnp.sin(angle_inner),
    )


def complex_weights(cos_part, sin_part, real_only=False):
    top = jnp.concatenate([cos_part, sin_part], axis=1)
    bottom = jnp.concatenate([-sin_part, cos_part], axis=1)
    if real_only:
        return jnp.stack([cos_part, -sin_part])
    return jnp.stack([top, bottom])


def transform_last(real_part, imag_part):
    row_total, length = real_part.shape
    outer_len = 32
    inner_len = length // outer_len
    cos_outer, sin_outer, cos_twist, sin_twist, cos_inner, sin_inner = dft_tables(length)
    product = partial(jnp.einsum, precision=lax.Precision.HIGH)
    both = jnp.stack([real_part, imag_part]).reshape(2, row_total, outer_len, inner_len)
    step = product("prab,pak->rkb", both, complex_weights(cos_outer, sin_outer))
    step_real = step[:, :outer_len]
    step_imag = step[:, outer_len:]
    twist_real = step_real * cos_twist - step_imag * sin_twist
    twist_imag = step_real * sin_twist + step_imag * cos_twist
    out = product(
        "qrkb,qbm->rmk",
        jnp.stack([twist_real, twist_imag]),
        complex_weights(cos_inner, sin_inner),
    )
    out_real = out[:, :inner_len].reshape(row_total, length)
    out_imag = out[:, inner_len:].reshape(row_total, length)
    return (out_real, out_imag)


def transform_first_real(both):
    _, length, col_total = both.shape
    outer_len = 32
    inner_len = length // outer_len
    cos_outer, sin_outer, cos_twist, sin_twist, cos_inner, sin_inner = dft_tables(length)
    product = partial(jnp.einsum, precision=lax.Precision.HIGH)
    both = both.reshape(2, outer_len, inner_len, col_total)
    step = product("pabc,pak->kbc", both, complex_weights(cos_outer, sin_outer))
    step_real = step[:outer_len]
    step_imag = step[outer_len:]
    twist_real = step_real * cos_twist[:, :, None] - step_imag * sin_twist[:, :, None]
    twist_imag = step_real * sin_twist[:, :, None] + step_imag * cos_twist[:, :, None]
    out_real = product(
        "qkbc,qbm->mkc",
        jnp.stack([twist_real, twist_imag]),
        complex_weights(cos_inner, sin_inner, real_only=True),
    )
    return out_real.reshape(length, col_total)


PAY_ROWS = 19


GROUP = 8


def grid_kernel(tile_ref, pay_ref, out_ref, order_ref):
    tiles_total = out_ref.shape[1] // TU * (out_ref.shape[2] // TV)
    tile_cols = out_ref.shape[2] // TV
    lanes = pay_ref.shape[2]
    out_ref[...] = jnp.zeros(out_ref.shape, jnp.float32)
    du_base = lax.broadcasted_iota(jnp.int32, (TU, lanes), 0)
    dv_base = lax.broadcasted_iota(jnp.int32, (TV, lanes), 0).astype(jnp.bfloat16)

    def one_block(slot):
        blk = pay_ref[slot].astype(jnp.float32)
        vis = blk[0:2]
        ku = blk[2:9]
        ou = blk[16:17].astype(jnp.int32)
        du = du_base - ou
        su = jnp.zeros((TU, lanes), jnp.float32)
        for t in range(7):
            su = jnp.where(du == t, ku[t : t + 1], su)
        left = jnp.concatenate([vis[0:1] * su, vis[1:2] * su], axis=0).astype(jnp.bfloat16)
        raw = pay_ref[slot]
        dv = dv_base - raw[17:18]
        sv = jnp.zeros((TV, lanes), jnp.bfloat16)
        for t in range(7):
            sv = jnp.where(dv == t, raw[9 + t : 10 + t], sv)
        return lax.dot_general(
            left, sv, (((1,), (1,)), ((), ())), preferred_element_type=jnp.float32
        )

    def fill(s, filled):
        order_ref[filled] = s
        return filled + (tile_ref[s] < tiles_total).astype(jnp.int32)

    count = lax.fori_loop(0, pay_ref.shape[0], fill, jnp.int32(0))

    def body(i, carry):
        places = [i * GROUP + g for g in range(GROUP)]
        slots = [order_ref[jnp.minimum(q, count - 1)] for q in places]
        contribs = [one_block(s) for s in slots]
        for q, s, contrib in zip(places, slots, contribs):
            tile = jnp.minimum(tile_ref[s], tiles_total - 1)
            row0 = pl.multiple_of((tile // tile_cols) * TU, TU)
            col0 = pl.multiple_of((tile % tile_cols) * TV, TV)

            @pl.when(q < count)
            def _():
                for p in range(2):
                    out_ref[p, pl.ds(row0, TU), pl.ds(col0, TV)] += contrib[
                        p * TU : (p + 1) * TU
                    ]
        return carry

    steps = (count + GROUP - 1) // GROUP
    lax.fori_loop(0, steps, body, 0)


def grid_into_slab(tile_ids, payload, slab_rows):
    return pl.pallas_call(
        grid_kernel,
        out_shape=jax.ShapeDtypeStruct((2, slab_rows, GRID), jnp.float32),
        in_specs=[
            pl.BlockSpec(memory_space=pltpu.SMEM),
            pl.BlockSpec(memory_space=pltpu.VMEM),
        ],
        out_specs=pl.BlockSpec(memory_space=pltpu.VMEM),
        scratch_shapes=[pltpu.SMEM((payload.shape[0],), jnp.int32)],
    )(tile_ids, payload)


def shards(
    vis_values, kernel_u, kernel_v, offset_u, offset_v, block_owner, tile_slot, channel_freq
):
    row_count = lax.axis_size("row")
    block_count = vis_values.shape[1]
    vis_count = vis_values.shape[3]
    capacity = max(2, 4 * block_count // row_count)
    slot_count = row_count * capacity
    slab_rows = GRID // row_count
    tiles_total = slab_rows // TU * (GRID // TV)
    owner_row = block_owner[0, :, 0]
    row_marks = (owner_row[:, None] == jnp.arange(row_count, dtype=jnp.int32)[None, :]).astype(
        jnp.int32
    )
    before = jnp.cumsum(row_marks, axis=0) - row_marks
    slot_rank = jnp.sum(before * row_marks, axis=1)
    target = owner_row * capacity + slot_rank
    tile_row = jnp.broadcast_to(
        tile_slot[0][:, None, None].astype(jnp.bfloat16), (block_count, 1, vis_count)
    )
    payload = jnp.concatenate(
        [
            vis_values[0],
            kernel_u[0],
            kernel_v[0],
            offset_u[0][:, None, :].astype(jnp.bfloat16),
            offset_v[0][:, None, :].astype(jnp.bfloat16),
            tile_row,
        ],
        axis=1,
    )
    pick = (target[None, :] == jnp.arange(slot_count, dtype=jnp.int32)[:, None]).astype(
        jnp.bfloat16
    )
    send = jnp.einsum(
        "sb,bkn->skn", pick, payload, preferred_element_type=jnp.float32
    )
    empty = 1.0 - jnp.sum(pick.astype(jnp.float32), axis=1)
    send = send.at[:, PAY_ROWS - 1, :].add(empty[:, None] * tiles_total)
    send = send.astype(jnp.bfloat16)
    recv = lax.all_to_all(
        send.reshape((row_count, capacity) + payload.shape[1:]),
        "row",
        split_axis=0,
        concat_axis=0,
        tiled=True,
    ).reshape((slot_count,) + payload.shape[1:])
    tile_ids = jnp.max(recv[:, PAY_ROWS - 1, :].astype(jnp.float32), axis=1).astype(jnp.int32)
    slab_grid = grid_into_slab(tile_ids, recv, slab_rows)
    spec_real, spec_imag = transform_last(slab_grid[0], slab_grid[1])
    spectrum = jnp.stack([spec_real, spec_imag]).reshape(2, slab_rows, row_count, GRID // row_count)
    image_scale = 1.0 / math.sqrt(block_count * row_count * vis_count)
    offset_freq = (channel_freq[0] - 1.284) / 0.428
    weights = jnp.stack([jnp.ones_like(offset_freq), offset_freq, offset_freq * offset_freq])
    received = lax.all_to_all(
        for_sending(spectrum), "row", split_axis=2, concat_axis=1, tiled=True
    ).astype(spectrum.dtype)
    width_here = received.shape[2] * received.shape[3]
    dirty_image = transform_first_real(received.reshape(2, GRID, width_here)) * image_scale
    taylor_terms = (weights[:, None, None] * dirty_image[None]).astype(jnp.bfloat16)
    chips = lax.axis_size("z")
    pair = lax.axis_size("core")
    core = lax.axis_index("core")
    terms = taylor_terms.reshape(3, chips, pair, GRID // chips // pair, width_here)
    keep = lax.dynamic_index_in_dim(terms, core, axis=2, keepdims=False)
    give = lax.dynamic_index_in_dim(terms, pair - 1 - core, axis=2, keepdims=False)
    got = lax.ppermute(give, "core", [(0, 1), (1, 0)])
    partial_sum = (keep.astype(jnp.float32) + got.astype(jnp.float32)).astype(jnp.bfloat16)
    summed = lax.psum_scatter(partial_sum, "z", scatter_dimension=1, tiled=True)
    summed = summed.reshape(3, GRID // chips // pair, width_here)
    return summed


def solution(mesh):
    chips = mesh.shape["freq"] // 2
    split = Mesh(mesh.devices.reshape(chips, 2, mesh.shape["row"]), ("z", "core", "row"))
    freq = ("z", "core")
    return jax.shard_map(
        shards,
        mesh=split,
        in_specs=(
            P(freq, "row", None, None),
            P(freq, "row", None, None),
            P(freq, "row", None, None),
            P(freq, "row", None),
            P(freq, "row", None),
            P(freq, "row", None),
            P(freq, "row"),
            P(freq),
        ),
        out_specs=P(None, freq, "row"),
        check_vma=False,
    )
```

```python
from functools import partial
import math

import jax
import jax.numpy as jnp
from jax import lax
from jax.sharding import Mesh, PartitionSpec as P
from jax.experimental import pallas as pl
from jax.experimental.pallas import tpu as pltpu

GRID = 4096
TU = 16
TV = 128


def for_sending(shard):
    return jax.tree.map(lambda a: a.astype(jnp.bfloat16) if a.dtype == jnp.float32 else a, shard)


def dft_tables(length):
    outer_len = 32
    inner_len = length // outer_len
    index_outer = jnp.arange(outer_len, dtype=jnp.int32)
    index_inner = jnp.arange(inner_len, dtype=jnp.int32)
    full_turn = 2.0 * math.pi
    angle_outer = (
        full_turn
        * (index_outer[:, None] * index_outer[None, :] % outer_len).astype(jnp.float32)
        / outer_len
    )
    angle_twist = (
        full_turn
        * (index_outer[:, None] * index_inner[None, :] % length).astype(jnp.float32)
        / length
    )
    angle_inner = (
        full_turn
        * (index_inner[:, None] * index_inner[None, :] % inner_len).astype(jnp.float32)
        / inner_len
    )
    return (
        jnp.cos(angle_outer),
        jnp.sin(angle_outer),
        jnp.cos(angle_twist),
        jnp.sin(angle_twist),
        jnp.cos(angle_inner),
        jnp.sin(angle_inner),
    )


def complex_weights(cos_part, sin_part, real_only=False):
    top = jnp.concatenate([cos_part, sin_part], axis=1)
    bottom = jnp.concatenate([-sin_part, cos_part], axis=1)
    if real_only:
        return jnp.stack([cos_part, -sin_part])
    return jnp.stack([top, bottom])


def transform_last(both):
    _, outer_len, row_total, inner_len = both.shape
    length = outer_len * inner_len
    cos_outer, sin_outer, cos_twist, sin_twist, cos_inner, sin_inner = dft_tables(length)
    product = partial(jnp.einsum, precision=lax.Precision.HIGH)
    step = product("parb,pak->krb", both, complex_weights(cos_outer, sin_outer))
    step_real = step[:outer_len]
    step_imag = step[outer_len:]
    twist_real = step_real * cos_twist[:, None, :] - step_imag * sin_twist[:, None, :]
    twist_imag = step_real * sin_twist[:, None, :] + step_imag * cos_twist[:, None, :]
    chunks = length // CHUNK
    weights = complex_weights(cos_inner, sin_inner).reshape(
        2, inner_len, 2, chunks, inner_len // chunks
    )
    out = product("qkrb,qbsdm->drsmk", jnp.stack([twist_real, twist_imag]), weights)
    return out.reshape(chunks, row_total, 2, CHUNK)


def transform_first_real(both):
    outer_len, inner_len, _, col_total = both.shape
    length = outer_len * inner_len
    cos_outer, sin_outer, cos_twist, sin_twist, cos_inner, sin_inner = dft_tables(length)
    product = partial(jnp.einsum, precision=lax.Precision.HIGH)
    step = product("abpc,pak->kbc", both, complex_weights(cos_outer, sin_outer))
    step_real = step[:outer_len]
    step_imag = step[outer_len:]
    twist_real = step_real * cos_twist[:, :, None] - step_imag * sin_twist[:, :, None]
    twist_imag = step_real * sin_twist[:, :, None] + step_imag * cos_twist[:, :, None]
    out_real = product(
        "qkbc,qbm->mkc",
        jnp.stack([twist_real, twist_imag]),
        complex_weights(cos_inner, sin_inner, real_only=True),
    )
    return out_real.reshape(length, col_total)


PAY_ROWS = 19
CHUNK = 128


GROUP = 8


def grid_kernel(tile_ref, pay_ref, out_ref, order_ref):
    tiles_total = out_ref.shape[2] // TU * out_ref.shape[1]
    tile_cols = out_ref.shape[1]
    lanes = pay_ref.shape[2]
    out_ref[...] = jnp.zeros(out_ref.shape, jnp.float32)
    du_base = lax.broadcasted_iota(jnp.int32, (TU, lanes), 0)
    dv_base = lax.broadcasted_iota(jnp.int32, (TV, lanes), 0).astype(jnp.bfloat16)

    def one_block(slot):
        blk = pay_ref[slot].astype(jnp.float32)
        vis = blk[0:2]
        ku = blk[2:9]
        ou = blk[16:17].astype(jnp.int32)
        du = du_base - ou
        su = jnp.zeros((TU, lanes), jnp.float32)
        for t in range(7):
            su = jnp.where(du == t, ku[t : t + 1], su)
        left = jnp.concatenate([vis[0:1] * su, vis[1:2] * su], axis=0).astype(jnp.bfloat16)
        raw = pay_ref[slot]
        dv = dv_base - raw[17:18]
        sv = jnp.zeros((TV, lanes), jnp.bfloat16)
        for t in range(7):
            sv = jnp.where(dv == t, raw[9 + t : 10 + t], sv)
        return lax.dot_general(
            left, sv, (((1,), (1,)), ((), ())), preferred_element_type=jnp.float32
        )

    def fill(s, filled):
        order_ref[filled] = s
        return filled + (tile_ref[s] < tiles_total).astype(jnp.int32)

    count = lax.fori_loop(0, pay_ref.shape[0], fill, jnp.int32(0))

    def body(i, carry):
        places = [i * GROUP + g for g in range(GROUP)]
        slots = [order_ref[jnp.minimum(q, count - 1)] for q in places]
        contribs = [one_block(s) for s in slots]
        for q, s, contrib in zip(places, slots, contribs):
            tile = jnp.minimum(tile_ref[s], tiles_total - 1)
            row0 = pl.multiple_of((tile // tile_cols) * TU, TU)
            col = tile % tile_cols

            @pl.when(q < count)
            def _():
                for p in range(2):
                    out_ref[p, col, pl.ds(row0, TU), :] += contrib[p * TU : (p + 1) * TU]
        return carry

    steps = (count + GROUP - 1) // GROUP
    lax.fori_loop(0, steps, body, 0)


def grid_into_slab(tile_ids, payload, slab_rows):
    return pl.pallas_call(
        grid_kernel,
        out_shape=jax.ShapeDtypeStruct((2, GRID // TV, slab_rows, TV), jnp.float32),
        in_specs=[
            pl.BlockSpec(memory_space=pltpu.SMEM),
            pl.BlockSpec(memory_space=pltpu.VMEM),
        ],
        out_specs=pl.BlockSpec(memory_space=pltpu.VMEM),
        scratch_shapes=[pltpu.SMEM((payload.shape[0],), jnp.int32)],
    )(tile_ids, payload)


def shards(
    vis_values, kernel_u, kernel_v, offset_u, offset_v, block_owner, tile_slot, channel_freq
):
    row_count = lax.axis_size("row")
    block_count = vis_values.shape[1]
    vis_count = vis_values.shape[3]
    capacity = max(2, 4 * block_count // row_count)
    slot_count = row_count * capacity
    slab_rows = GRID // row_count
    tiles_total = slab_rows // TU * (GRID // TV)
    owner_row = block_owner[0, :, 0]
    row_marks = (owner_row[:, None] == jnp.arange(row_count, dtype=jnp.int32)[None, :]).astype(
        jnp.int32
    )
    before = jnp.cumsum(row_marks, axis=0) - row_marks
    slot_rank = jnp.sum(before * row_marks, axis=1)
    target = owner_row * capacity + slot_rank
    tile_row = jnp.broadcast_to(
        tile_slot[0][:, None, None].astype(jnp.bfloat16), (block_count, 1, vis_count)
    )
    payload = jnp.concatenate(
        [
            vis_values[0],
            kernel_u[0],
            kernel_v[0],
            offset_u[0][:, None, :].astype(jnp.bfloat16),
            offset_v[0][:, None, :].astype(jnp.bfloat16),
            tile_row,
        ],
        axis=1,
    )
    pick = (target[None, :] == jnp.arange(slot_count, dtype=jnp.int32)[:, None]).astype(
        jnp.bfloat16
    )
    send = jnp.einsum(
        "sb,bkn->skn", pick, payload, preferred_element_type=jnp.float32
    )
    empty = 1.0 - jnp.sum(pick.astype(jnp.float32), axis=1)
    send = send.at[:, PAY_ROWS - 1, :].add(empty[:, None] * tiles_total)
    send = send.astype(jnp.bfloat16)
    recv = lax.all_to_all(
        send.reshape((row_count, capacity) + payload.shape[1:]),
        "row",
        split_axis=0,
        concat_axis=0,
        tiled=True,
    ).reshape((slot_count,) + payload.shape[1:])
    tile_ids = jnp.max(recv[:, PAY_ROWS - 1, :].astype(jnp.float32), axis=1).astype(jnp.int32)
    slab_grid = grid_into_slab(tile_ids, recv, slab_rows)
    spectrum = transform_last(slab_grid)
    image_scale = 1.0 / math.sqrt(block_count * row_count * vis_count)
    offset_freq = (channel_freq[0] - 1.284) / 0.428
    weights = jnp.stack([jnp.ones_like(offset_freq), offset_freq, offset_freq * offset_freq])
    received = lax.all_to_all(
        for_sending(spectrum), "row", split_axis=0, concat_axis=0, tiled=True
    ).astype(spectrum.dtype)
    width_here = received.shape[3]
    dirty_image = transform_first_real(received) * image_scale
    taylor_terms = (weights[:, None, None] * dirty_image[None]).astype(jnp.bfloat16)
    chips = lax.axis_size("z")
    pair = lax.axis_size("core")
    core = lax.axis_index("core")
    terms = taylor_terms.reshape(3, chips, pair, GRID // chips // pair, width_here)
    keep = lax.dynamic_index_in_dim(terms, core, axis=2, keepdims=False)
    give = lax.dynamic_index_in_dim(terms, pair - 1 - core, axis=2, keepdims=False)
    got = lax.ppermute(give, "core", [(0, 1), (1, 0)])
    partial_sum = (keep.astype(jnp.float32) + got.astype(jnp.float32)).astype(jnp.bfloat16)
    summed = lax.psum_scatter(partial_sum, "z", scatter_dimension=1, tiled=True)
    summed = summed.reshape(3, GRID // chips // pair, width_here)
    return summed


def solution(mesh):
    chips = mesh.shape["freq"] // 2
    split = Mesh(mesh.devices.reshape(chips, 2, mesh.shape["row"]), ("z", "core", "row"))
    freq = ("z", "core")
    return jax.shard_map(
        shards,
        mesh=split,
        in_specs=(
            P(freq, "row", None, None),
            P(freq, "row", None, None),
            P(freq, "row", None, None),
            P(freq, "row", None),
            P(freq, "row", None),
            P(freq, "row", None),
            P(freq, "row"),
            P(freq),
        ),
        out_specs=P(None, freq, "row"),
        check_vma=False,
    )
```

```python
from functools import partial
import math

import jax
import jax.numpy as jnp
from jax import lax
from jax.sharding import Mesh, PartitionSpec as P
from jax.experimental import pallas as pl
from jax.experimental.pallas import tpu as pltpu

GRID = 4096
TU = 16
TV = 128


def for_sending(shard):
    return jax.tree.map(lambda a: a.astype(jnp.bfloat16) if a.dtype == jnp.float32 else a, shard)


def dft_tables(length):
    outer_len = 32
    inner_len = length // outer_len
    index_outer = jnp.arange(outer_len, dtype=jnp.int32)
    index_inner = jnp.arange(inner_len, dtype=jnp.int32)
    full_turn = 2.0 * math.pi
    angle_outer = (
        full_turn
        * (index_outer[:, None] * index_outer[None, :] % outer_len).astype(jnp.float32)
        / outer_len
    )
    angle_twist = (
        full_turn
        * (index_outer[:, None] * index_inner[None, :] % length).astype(jnp.float32)
        / length
    )
    angle_inner = (
        full_turn
        * (index_inner[:, None] * index_inner[None, :] % inner_len).astype(jnp.float32)
        / inner_len
    )
    return (
        jnp.cos(angle_outer),
        jnp.sin(angle_outer),
        jnp.cos(angle_twist),
        jnp.sin(angle_twist),
        jnp.cos(angle_inner),
        jnp.sin(angle_inner),
    )


def complex_weights(cos_part, sin_part, real_only=False):
    top = jnp.concatenate([cos_part, sin_part], axis=1)
    bottom = jnp.concatenate([-sin_part, cos_part], axis=1)
    if real_only:
        return jnp.stack([cos_part, -sin_part])
    return jnp.stack([top, bottom])


def transform_last(both):
    _, outer_len, row_total, inner_len = both.shape
    length = outer_len * inner_len
    cos_outer, sin_outer, cos_twist, sin_twist, cos_inner, sin_inner = dft_tables(length)
    product = partial(jnp.einsum, precision=lax.Precision.HIGH)
    step = product("parb,pak->krb", both, complex_weights(cos_outer, sin_outer))
    step_real = step[:outer_len]
    step_imag = step[outer_len:]
    twist_real = step_real * cos_twist[:, None, :] - step_imag * sin_twist[:, None, :]
    twist_imag = step_real * sin_twist[:, None, :] + step_imag * cos_twist[:, None, :]
    chunks = length // CHUNK
    weights = complex_weights(cos_inner, sin_inner).reshape(
        2, inner_len, 2, chunks, inner_len // chunks
    )
    out = product("qkrb,qbsdm->drsmk", jnp.stack([twist_real, twist_imag]), weights)
    return out.reshape(chunks, row_total, 2, CHUNK)


def transform_first_real(both):
    outer_len, inner_len, _, col_total = both.shape
    length = outer_len * inner_len
    cos_outer, sin_outer, cos_twist, sin_twist, cos_inner, sin_inner = dft_tables(length)
    product = partial(jnp.einsum, precision=lax.Precision.HIGH)
    step = product("abpc,pak->kbc", both, complex_weights(cos_outer, sin_outer))
    step_real = step[:outer_len]
    step_imag = step[outer_len:]
    twist_real = step_real * cos_twist[:, :, None] - step_imag * sin_twist[:, :, None]
    twist_imag = step_real * sin_twist[:, :, None] + step_imag * cos_twist[:, :, None]
    out_real = product(
        "qkbc,qbm->mkc",
        jnp.stack([twist_real, twist_imag]),
        complex_weights(cos_inner, sin_inner, real_only=True),
    )
    return out_real.reshape(length, col_total)


PAY_ROWS = 19
CHUNK = 128


GROUP = 8


def grid_kernel(tile_ref, pay_ref, out_ref, order_ref):
    tiles_total = out_ref.shape[2] // TU * out_ref.shape[1]
    tile_cols = out_ref.shape[1]
    lanes = pay_ref.shape[2]
    out_ref[...] = jnp.zeros(out_ref.shape, jnp.float32)
    du_base = lax.broadcasted_iota(jnp.int32, (TU, lanes), 0)
    dv_base = lax.broadcasted_iota(jnp.int32, (TV, lanes), 0).astype(jnp.bfloat16)

    def one_block(slot):
        blk = pay_ref[slot].astype(jnp.float32)
        vis = blk[0:2]
        ku = blk[2:9]
        ou = blk[16:17].astype(jnp.int32)
        du = du_base - ou
        su = jnp.zeros((TU, lanes), jnp.float32)
        for t in range(7):
            su = jnp.where(du == t, ku[t : t + 1], su)
        left = jnp.concatenate([vis[0:1] * su, vis[1:2] * su], axis=0).astype(jnp.bfloat16)
        raw = pay_ref[slot]
        dv = dv_base - raw[17:18]
        sv = jnp.zeros((TV, lanes), jnp.bfloat16)
        for t in range(7):
            sv = jnp.where(dv == t, raw[9 + t : 10 + t], sv)
        return lax.dot_general(
            left, sv, (((1,), (1,)), ((), ())), preferred_element_type=jnp.float32
        )

    def fill(s, filled):
        order_ref[filled] = s
        return filled + (tile_ref[s] < tiles_total).astype(jnp.int32)

    count = lax.fori_loop(0, pay_ref.shape[0], fill, jnp.int32(0))

    def body(i, carry):
        places = [i * GROUP + g for g in range(GROUP)]
        slots = [order_ref[jnp.minimum(q, count - 1)] for q in places]
        contribs = [one_block(s) for s in slots]
        for q, s, contrib in zip(places, slots, contribs):
            tile = jnp.minimum(tile_ref[s], tiles_total - 1)
            row0 = pl.multiple_of((tile // tile_cols) * TU, TU)
            col = tile % tile_cols

            @pl.when(q < count)
            def _():
                for p in range(2):
                    out_ref[p, col, pl.ds(row0, TU), :] += contrib[p * TU : (p + 1) * TU]
        return carry

    steps = (count + GROUP - 1) // GROUP
    lax.fori_loop(0, steps, body, 0)


def grid_into_slab(tile_ids, payload, slab_rows):
    return pl.pallas_call(
        grid_kernel,
        out_shape=jax.ShapeDtypeStruct((2, GRID // TV, slab_rows, TV), jnp.float32),
        in_specs=[
            pl.BlockSpec(memory_space=pltpu.SMEM),
            pl.BlockSpec(memory_space=pltpu.VMEM),
        ],
        out_specs=pl.BlockSpec(memory_space=pltpu.VMEM),
        scratch_shapes=[pltpu.SMEM((payload.shape[0],), jnp.int32)],
    )(tile_ids, payload)


def shards(
    vis_values, kernel_u, kernel_v, offset_u, offset_v, block_owner, tile_slot, channel_freq
):
    row_count = lax.axis_size("row")
    block_count = vis_values.shape[1]
    vis_count = vis_values.shape[3]
    capacity = max(2, 4 * block_count // row_count)
    slot_count = row_count * capacity
    slab_rows = GRID // row_count
    tiles_total = slab_rows // TU * (GRID // TV)
    owner_row = block_owner[0, :, 0]
    row_marks = (owner_row[:, None] == jnp.arange(row_count, dtype=jnp.int32)[None, :]).astype(
        jnp.int32
    )
    before = jnp.cumsum(row_marks, axis=0) - row_marks
    slot_rank = jnp.sum(before * row_marks, axis=1)
    target = owner_row * capacity + slot_rank
    tile_row = jnp.broadcast_to(
        tile_slot[0][:, None, None].astype(jnp.bfloat16), (block_count, 1, vis_count)
    )
    payload = jnp.concatenate(
        [
            vis_values[0],
            kernel_u[0],
            kernel_v[0],
            offset_u[0][:, None, :].astype(jnp.bfloat16),
            offset_v[0][:, None, :].astype(jnp.bfloat16),
            tile_row,
        ],
        axis=1,
    )
    pick = (target[None, :] == jnp.arange(slot_count, dtype=jnp.int32)[:, None]).astype(
        jnp.bfloat16
    )
    send = jnp.einsum(
        "sb,bkn->skn", pick, payload, preferred_element_type=jnp.float32
    )
    empty = 1.0 - jnp.sum(pick.astype(jnp.float32), axis=1)
    send = send.at[:, PAY_ROWS - 1, :].add(empty[:, None] * tiles_total)
    send = send.astype(jnp.bfloat16)
    recv = lax.all_to_all(
        send.reshape((row_count, capacity) + payload.shape[1:]),
        "row",
        split_axis=0,
        concat_axis=0,
        tiled=True,
    ).reshape((slot_count,) + payload.shape[1:])
    tile_ids = jnp.max(recv[:, PAY_ROWS - 1, :].astype(jnp.float32), axis=1).astype(jnp.int32)
    slab_grid = grid_into_slab(tile_ids, recv, slab_rows)
    spectrum = transform_last(slab_grid)
    image_scale = 1.0 / math.sqrt(block_count * row_count * vis_count)
    offset_freq = (channel_freq[0] - 1.284) / 0.428
    weights = jnp.stack([jnp.ones_like(offset_freq), offset_freq, offset_freq * offset_freq])
    received = lax.all_to_all(
        for_sending(spectrum), "row", split_axis=0, concat_axis=0, tiled=True
    ).astype(spectrum.dtype)
    width_here = received.shape[3]
    dirty_image = transform_first_real(received) * image_scale
    chips = lax.axis_size("z")
    pair = lax.axis_size("core")
    core = lax.axis_index("core")
    halves = dirty_image.reshape(chips, pair, GRID // chips // pair, width_here)
    keep = lax.dynamic_index_in_dim(halves, core, axis=1, keepdims=False)
    give = lax.dynamic_index_in_dim(halves, pair - 1 - core, axis=1, keepdims=False)
    swap = [(0, 1), (1, 0)]
    got = lax.ppermute(give, "core", swap)
    got_weights = lax.ppermute(weights, "core", swap)
    mine = (weights[:, None, None, None] * keep[None]).astype(jnp.bfloat16)
    theirs = (got_weights[:, None, None, None] * got[None]).astype(jnp.bfloat16)
    partial_sum = (mine.astype(jnp.float32) + theirs.astype(jnp.float32)).astype(jnp.bfloat16)
    summed = lax.psum_scatter(partial_sum, "z", scatter_dimension=1, tiled=True)
    summed = summed.reshape(3, GRID // chips // pair, width_here)
    return summed


def solution(mesh):
    chips = mesh.shape["freq"] // 2
    split = Mesh(mesh.devices.reshape(chips, 2, mesh.shape["row"]), ("z", "core", "row"))
    freq = ("z", "core")
    return jax.shard_map(
        shards,
        mesh=split,
        in_specs=(
            P(freq, "row", None, None),
            P(freq, "row", None, None),
            P(freq, "row", None, None),
            P(freq, "row", None),
            P(freq, "row", None),
            P(freq, "row", None),
            P(freq, "row"),
            P(freq),
        ),
        out_specs=P(None, freq, "row"),
        check_vma=False,
    )
```

```python
from functools import partial
import math

import jax
import jax.numpy as jnp
from jax import lax
from jax.sharding import Mesh, PartitionSpec as P
from jax.experimental import pallas as pl
from jax.experimental.pallas import tpu as pltpu

GRID = 4096
TU = 16
TV = 128


def for_sending(shard):
    return jax.tree.map(lambda a: a.astype(jnp.bfloat16) if a.dtype == jnp.float32 else a, shard)


def dft_tables(length):
    outer_len = 32
    inner_len = length // outer_len
    index_outer = jnp.arange(outer_len, dtype=jnp.int32)
    index_inner = jnp.arange(inner_len, dtype=jnp.int32)
    full_turn = 2.0 * math.pi
    angle_outer = (
        full_turn
        * (index_outer[:, None] * index_outer[None, :] % outer_len).astype(jnp.float32)
        / outer_len
    )
    angle_twist = (
        full_turn
        * (index_outer[:, None] * index_inner[None, :] % length).astype(jnp.float32)
        / length
    )
    angle_inner = (
        full_turn
        * (index_inner[:, None] * index_inner[None, :] % inner_len).astype(jnp.float32)
        / inner_len
    )
    return (
        jnp.cos(angle_outer),
        jnp.sin(angle_outer),
        jnp.cos(angle_twist),
        jnp.sin(angle_twist),
        jnp.cos(angle_inner),
        jnp.sin(angle_inner),
    )


def complex_weights(cos_part, sin_part, real_only=False):
    top = jnp.concatenate([cos_part, sin_part], axis=1)
    bottom = jnp.concatenate([-sin_part, cos_part], axis=1)
    if real_only:
        return jnp.stack([cos_part, -sin_part])
    return jnp.stack([top, bottom])


def transform_last(both):
    _, outer_len, row_total, inner_len = both.shape
    length = outer_len * inner_len
    cos_outer, sin_outer, cos_twist, sin_twist, cos_inner, sin_inner = dft_tables(length)
    product = partial(jnp.einsum, precision=lax.Precision.HIGH)
    step = product("parb,pak->krb", both, complex_weights(cos_outer, sin_outer))
    step_real = step[:outer_len]
    step_imag = step[outer_len:]
    twist_real = step_real * cos_twist[:, None, :] - step_imag * sin_twist[:, None, :]
    twist_imag = step_real * sin_twist[:, None, :] + step_imag * cos_twist[:, None, :]
    chunks = length // CHUNK
    weights = complex_weights(cos_inner, sin_inner).reshape(
        2, inner_len, 2, chunks, inner_len // chunks
    )
    out = product("qkrb,qbsdm->drsmk", jnp.stack([twist_real, twist_imag]), weights)
    return out.reshape(chunks, row_total, 2, CHUNK)


def transform_first_real(both):
    outer_len, inner_len, _, col_total = both.shape
    length = outer_len * inner_len
    cos_outer, sin_outer, cos_twist, sin_twist, cos_inner, sin_inner = dft_tables(length)
    product = partial(jnp.einsum, precision=lax.Precision.HIGH)
    step = product("abpc,pak->kbc", both, complex_weights(cos_outer, sin_outer))
    step_real = step[:outer_len]
    step_imag = step[outer_len:]
    twist_real = step_real * cos_twist[:, :, None] - step_imag * sin_twist[:, :, None]
    twist_imag = step_real * sin_twist[:, :, None] + step_imag * cos_twist[:, :, None]
    out_real = product(
        "qkbc,qbm->mkc",
        jnp.stack([twist_real, twist_imag]),
        complex_weights(cos_inner, sin_inner, real_only=True),
    )
    return out_real.reshape(length, col_total)


PAY_ROWS = 19
CHUNK = 128


GROUP = 8


def grid_kernel(tile_ref, pay_ref, out_ref, order_ref):
    tiles_total = out_ref.shape[2] // TU * out_ref.shape[1]
    tile_cols = out_ref.shape[1]
    lanes = pay_ref.shape[2]
    out_ref[...] = jnp.zeros(out_ref.shape, jnp.float32)
    du_base = lax.broadcasted_iota(jnp.int32, (TU, lanes), 0)
    dv_base = lax.broadcasted_iota(jnp.int32, (TV, lanes), 0).astype(jnp.bfloat16)

    def one_block(slot):
        blk = pay_ref[slot].astype(jnp.float32)
        vis = blk[0:2]
        ku = blk[2:9]
        ou = blk[16:17].astype(jnp.int32)
        du = du_base - ou
        su = jnp.zeros((TU, lanes), jnp.float32)
        for t in range(7):
            su = jnp.where(du == t, ku[t : t + 1], su)
        left = jnp.concatenate([vis[0:1] * su, vis[1:2] * su], axis=0).astype(jnp.bfloat16)
        raw = pay_ref[slot]
        dv = dv_base - raw[17:18]
        sv = jnp.zeros((TV, lanes), jnp.bfloat16)
        for t in range(7):
            sv = jnp.where(dv == t, raw[9 + t : 10 + t], sv)
        return lax.dot_general(
            left, sv, (((1,), (1,)), ((), ())), preferred_element_type=jnp.float32
        )

    def fill(s, filled):
        order_ref[filled] = s
        return filled + (tile_ref[s] < tiles_total).astype(jnp.int32)

    count = lax.fori_loop(0, pay_ref.shape[0], fill, jnp.int32(0))

    def body(i, carry):
        places = [i * GROUP + g for g in range(GROUP)]
        slots = [order_ref[jnp.minimum(q, count - 1)] for q in places]
        contribs = [one_block(s) for s in slots]
        for q, s, contrib in zip(places, slots, contribs):
            tile = jnp.minimum(tile_ref[s], tiles_total - 1)
            row0 = pl.multiple_of((tile // tile_cols) * TU, TU)
            col = tile % tile_cols

            @pl.when(q < count)
            def _():
                for p in range(2):
                    out_ref[p, col, pl.ds(row0, TU), :] += contrib[p * TU : (p + 1) * TU]
        return carry

    steps = (count + GROUP - 1) // GROUP
    lax.fori_loop(0, steps, body, 0)


def grid_into_slab(tile_ids, payload, slab_rows):
    return pl.pallas_call(
        grid_kernel,
        out_shape=jax.ShapeDtypeStruct((2, GRID // TV, slab_rows, TV), jnp.float32),
        in_specs=[
            pl.BlockSpec(memory_space=pltpu.SMEM),
            pl.BlockSpec(memory_space=pltpu.VMEM),
        ],
        out_specs=pl.BlockSpec(memory_space=pltpu.VMEM),
        scratch_shapes=[pltpu.SMEM((payload.shape[0],), jnp.int32)],
    )(tile_ids, payload)


def shards(
    vis_values, kernel_u, kernel_v, offset_u, offset_v, block_owner, tile_slot, channel_freq
):
    row_count = lax.axis_size("row")
    block_count = vis_values.shape[1]
    vis_count = vis_values.shape[3]
    capacity = max(2, 4 * block_count // row_count)
    slot_count = row_count * capacity
    slab_rows = GRID // row_count
    tiles_total = slab_rows // TU * (GRID // TV)
    owner_row = block_owner[0, :, 0]
    row_marks = (owner_row[:, None] == jnp.arange(row_count, dtype=jnp.int32)[None, :]).astype(
        jnp.int32
    )
    before = jnp.cumsum(row_marks, axis=0) - row_marks
    slot_rank = jnp.sum(before * row_marks, axis=1)
    target = owner_row * capacity + slot_rank
    tile_row = jnp.broadcast_to(
        tile_slot[0][:, None, None].astype(jnp.bfloat16), (block_count, 1, vis_count)
    )
    payload = jnp.concatenate(
        [
            vis_values[0],
            kernel_u[0],
            kernel_v[0],
            offset_u[0][:, None, :].astype(jnp.bfloat16),
            offset_v[0][:, None, :].astype(jnp.bfloat16),
            tile_row,
        ],
        axis=1,
    )
    pick = (target[None, :] == jnp.arange(slot_count, dtype=jnp.int32)[:, None]).astype(
        jnp.bfloat16
    )
    send = jnp.einsum(
        "sb,bkn->skn", pick, payload, preferred_element_type=jnp.float32
    )
    empty = 1.0 - jnp.sum(pick.astype(jnp.float32), axis=1)
    send = send.at[:, PAY_ROWS - 1, :].add(empty[:, None] * tiles_total)
    send = send.astype(jnp.bfloat16)
    recv = lax.all_to_all(
        send.reshape((row_count, capacity) + payload.shape[1:]),
        "row",
        split_axis=0,
        concat_axis=0,
        tiled=True,
    ).reshape((slot_count,) + payload.shape[1:])
    tile_ids = jnp.max(recv[:, PAY_ROWS - 1, :].astype(jnp.float32), axis=1).astype(jnp.int32)
    slab_grid = grid_into_slab(tile_ids, recv, slab_rows)
    spectrum = transform_last(slab_grid)
    image_scale = 1.0 / math.sqrt(block_count * row_count * vis_count)
    offset_freq = (channel_freq[0] - 1.284) / 0.428
    weights = jnp.stack([jnp.ones_like(offset_freq), offset_freq, offset_freq * offset_freq])
    received = lax.all_to_all(
        for_sending(spectrum), "row", split_axis=0, concat_axis=0, tiled=True
    ).astype(spectrum.dtype)
    width_here = received.shape[3]
    dirty_image = transform_first_real(received) * image_scale
    chips = lax.axis_size("z")
    pair = lax.axis_size("core")
    core = lax.axis_index("core")
    halves = dirty_image.reshape(chips, pair, GRID // chips // pair, width_here)
    keep = lax.dynamic_index_in_dim(halves, core, axis=1, keepdims=False)
    give = lax.dynamic_index_in_dim(halves, pair - 1 - core, axis=1, keepdims=False)
    swap = [(0, 1), (1, 0)]
    packed = jnp.concatenate([give.reshape(-1), weights])
    got_packed = lax.ppermute(packed, "core", swap)
    got = got_packed[: give.size].reshape(give.shape)
    got_weights = got_packed[give.size :]
    mine = (weights[:, None, None, None] * keep[None]).astype(jnp.bfloat16)
    theirs = (got_weights[:, None, None, None] * got[None]).astype(jnp.bfloat16)
    partial_sum = (mine.astype(jnp.float32) + theirs.astype(jnp.float32)).astype(jnp.bfloat16)
    summed = lax.psum_scatter(partial_sum, "z", scatter_dimension=1, tiled=True)
    summed = summed.reshape(3, GRID // chips // pair, width_here)
    return summed


def solution(mesh):
    chips = mesh.shape["freq"] // 2
    split = Mesh(mesh.devices.reshape(chips, 2, mesh.shape["row"]), ("z", "core", "row"))
    freq = ("z", "core")
    return jax.shard_map(
        shards,
        mesh=split,
        in_specs=(
            P(freq, "row", None, None),
            P(freq, "row", None, None),
            P(freq, "row", None, None),
            P(freq, "row", None),
            P(freq, "row", None),
            P(freq, "row", None),
            P(freq, "row"),
            P(freq),
        ),
        out_specs=P(None, freq, "row"),
        check_vma=False,
    )
```

```python
from functools import partial
import math

import jax
import jax.numpy as jnp
from jax import lax
from jax.sharding import Mesh, PartitionSpec as P
from jax.experimental import pallas as pl
from jax.experimental.pallas import tpu as pltpu

GRID = 4096
TU = 16
TV = 128


def for_sending(shard):
    return jax.tree.map(lambda a: a.astype(jnp.bfloat16) if a.dtype == jnp.float32 else a, shard)


def dft_tables(length):
    outer_len = 32
    inner_len = length // outer_len
    index_outer = jnp.arange(outer_len, dtype=jnp.int32)
    index_inner = jnp.arange(inner_len, dtype=jnp.int32)
    full_turn = 2.0 * math.pi
    angle_outer = (
        full_turn
        * (index_outer[:, None] * index_outer[None, :] % outer_len).astype(jnp.float32)
        / outer_len
    )
    angle_twist = (
        full_turn
        * (index_outer[:, None] * index_inner[None, :] % length).astype(jnp.float32)
        / length
    )
    angle_inner = (
        full_turn
        * (index_inner[:, None] * index_inner[None, :] % inner_len).astype(jnp.float32)
        / inner_len
    )
    return (
        jnp.cos(angle_outer),
        jnp.sin(angle_outer),
        jnp.cos(angle_twist),
        jnp.sin(angle_twist),
        jnp.cos(angle_inner),
        jnp.sin(angle_inner),
    )


def complex_weights(cos_part, sin_part, real_only=False):
    top = jnp.concatenate([cos_part, sin_part], axis=1)
    bottom = jnp.concatenate([-sin_part, cos_part], axis=1)
    if real_only:
        return jnp.stack([cos_part, -sin_part])
    return jnp.stack([top, bottom])


def transform_last(both):
    _, outer_len, row_total, inner_len = both.shape
    length = outer_len * inner_len
    cos_outer, sin_outer, cos_twist, sin_twist, cos_inner, sin_inner = dft_tables(length)
    product = partial(jnp.einsum, precision=lax.Precision.HIGH)
    step = product("parb,pak->krb", both, complex_weights(cos_outer, sin_outer))
    step_real = step[:outer_len]
    step_imag = step[outer_len:]
    twist_real = step_real * cos_twist[:, None, :] - step_imag * sin_twist[:, None, :]
    twist_imag = step_real * sin_twist[:, None, :] + step_imag * cos_twist[:, None, :]
    chunks = length // CHUNK
    weights = complex_weights(cos_inner, sin_inner).reshape(
        2, inner_len, 2, chunks, inner_len // chunks
    )
    out = product("qkrb,qbsdm->drsmk", jnp.stack([twist_real, twist_imag]), weights)
    return out.reshape(chunks, row_total, 2, CHUNK)


def transform_first_real(both):
    outer_len, inner_len, _, col_total = both.shape
    length = outer_len * inner_len
    cos_outer, sin_outer, cos_twist, sin_twist, cos_inner, sin_inner = dft_tables(length)
    product = partial(jnp.einsum, precision=lax.Precision.HIGH)
    step = product("abpc,pak->kbc", both, complex_weights(cos_outer, sin_outer))
    step_real = step[:outer_len]
    step_imag = step[outer_len:]
    twist_real = step_real * cos_twist[:, :, None] - step_imag * sin_twist[:, :, None]
    twist_imag = step_real * sin_twist[:, :, None] + step_imag * cos_twist[:, :, None]
    out_real = product(
        "qkbc,qbm->mkc",
        jnp.stack([twist_real, twist_imag]),
        complex_weights(cos_inner, sin_inner, real_only=True),
    )
    return out_real.reshape(length, col_total)


PAY_ROWS = 19
CHUNK = 128


GROUP = 8


def grid_kernel(tile_ref, pay_ref, out_ref, order_ref):
    tiles_total = out_ref.shape[2] // TU * out_ref.shape[1]
    tile_cols = out_ref.shape[1]
    lanes = pay_ref.shape[2]
    out_ref[...] = jnp.zeros(out_ref.shape, jnp.float32)
    du_base = lax.broadcasted_iota(jnp.int32, (TU, lanes), 0)
    dv_base = lax.broadcasted_iota(jnp.int32, (TV, lanes), 0).astype(jnp.bfloat16)

    def one_block(slot):
        blk = pay_ref[slot].astype(jnp.float32)
        vis = blk[0:2]
        ku = blk[2:9]
        ou = blk[16:17].astype(jnp.int32)
        du = du_base - ou
        su = jnp.zeros((TU, lanes), jnp.float32)
        for t in range(7):
            su = jnp.where(du == t, ku[t : t + 1], su)
        left = jnp.concatenate([vis[0:1] * su, vis[1:2] * su], axis=0).astype(jnp.bfloat16)
        raw = pay_ref[slot]
        dv = dv_base - raw[17:18]
        sv = jnp.zeros((TV, lanes), jnp.bfloat16)
        for t in range(7):
            sv = jnp.where(dv == t, raw[9 + t : 10 + t], sv)
        return lax.dot_general(
            left, sv, (((1,), (1,)), ((), ())), preferred_element_type=jnp.float32
        )

    def fill(s, filled):
        order_ref[filled] = s
        return filled + (tile_ref[s] < tiles_total).astype(jnp.int32)

    count = lax.fori_loop(0, pay_ref.shape[0], fill, jnp.int32(0))

    def body(i, carry):
        places = [i * GROUP + g for g in range(GROUP)]
        slots = [order_ref[jnp.minimum(q, count - 1)] for q in places]
        contribs = [one_block(s) for s in slots]
        for q, s, contrib in zip(places, slots, contribs):
            tile = jnp.minimum(tile_ref[s], tiles_total - 1)
            row0 = pl.multiple_of((tile // tile_cols) * TU, TU)
            col = tile % tile_cols

            @pl.when(q < count)
            def _():
                for p in range(2):
                    out_ref[p, col, pl.ds(row0, TU), :] += contrib[p * TU : (p + 1) * TU]
        return carry

    steps = (count + GROUP - 1) // GROUP
    lax.fori_loop(0, steps, body, 0)


def grid_into_slab(tile_ids, payload, slab_rows):
    return pl.pallas_call(
        grid_kernel,
        out_shape=jax.ShapeDtypeStruct((2, GRID // TV, slab_rows, TV), jnp.float32),
        in_specs=[
            pl.BlockSpec(memory_space=pltpu.SMEM),
            pl.BlockSpec(memory_space=pltpu.VMEM),
        ],
        out_specs=pl.BlockSpec(memory_space=pltpu.VMEM),
        scratch_shapes=[pltpu.SMEM((payload.shape[0],), jnp.int32)],
    )(tile_ids, payload)


def shards(
    vis_values, kernel_u, kernel_v, offset_u, offset_v, block_owner, tile_slot, channel_freq
):
    row_count = lax.axis_size("row")
    block_count = vis_values.shape[1]
    vis_count = vis_values.shape[3]
    capacity = max(2, 4 * block_count // row_count)
    slot_count = row_count * capacity
    slab_rows = GRID // row_count
    tiles_total = slab_rows // TU * (GRID // TV)
    owner_row = block_owner[0, :, 0]
    row_marks = (owner_row[:, None] == jnp.arange(row_count, dtype=jnp.int32)[None, :]).astype(
        jnp.int32
    )
    before = jnp.cumsum(row_marks, axis=0) - row_marks
    slot_rank = jnp.sum(before * row_marks, axis=1)
    target = owner_row * capacity + slot_rank
    tile_row = jnp.broadcast_to(
        tile_slot[0][:, None, None].astype(jnp.bfloat16), (block_count, 1, vis_count)
    )
    payload = jnp.concatenate(
        [
            vis_values[0],
            kernel_u[0],
            kernel_v[0],
            offset_u[0][:, None, :].astype(jnp.bfloat16),
            offset_v[0][:, None, :].astype(jnp.bfloat16),
            tile_row,
        ],
        axis=1,
    )
    pick = (target[None, :] == jnp.arange(slot_count, dtype=jnp.int32)[:, None]).astype(
        jnp.bfloat16
    )
    send = jnp.einsum(
        "sb,bkn->skn", pick, payload, preferred_element_type=jnp.float32
    )
    empty = 1.0 - jnp.sum(pick.astype(jnp.float32), axis=1)
    send = send.at[:, PAY_ROWS - 1, :].add(empty[:, None] * tiles_total)
    send = send.astype(jnp.bfloat16)
    recv = lax.all_to_all(
        send.reshape((row_count, capacity) + payload.shape[1:]),
        "row",
        split_axis=0,
        concat_axis=0,
        tiled=True,
    ).reshape((slot_count,) + payload.shape[1:])
    tile_ids = jnp.max(recv[:, PAY_ROWS - 1, :].astype(jnp.float32), axis=1).astype(jnp.int32)
    slab_grid = grid_into_slab(tile_ids, recv, slab_rows)
    spectrum = transform_last(slab_grid)
    image_scale = 1.0 / math.sqrt(block_count * row_count * vis_count)
    def weights_of(frequency):
        offset = (frequency - 1.284) / 0.428
        return jnp.stack([jnp.ones_like(offset), offset, offset * offset])

    here = lax.axis_index("z") * lax.axis_size("core") + lax.axis_index("core")
    weights = weights_of(lax.dynamic_index_in_dim(channel_freq, here, keepdims=False))
    partner_weights = weights_of(
        lax.dynamic_index_in_dim(channel_freq, here + 1 - 2 * lax.axis_index("core"), keepdims=False)
    )
    received = lax.all_to_all(
        for_sending(spectrum), "row", split_axis=0, concat_axis=0, tiled=True
    ).astype(spectrum.dtype)
    width_here = received.shape[3]
    dirty_image = transform_first_real(received) * image_scale
    chips = lax.axis_size("z")
    pair = lax.axis_size("core")
    core = lax.axis_index("core")
    halves = dirty_image.reshape(chips, pair, GRID // chips // pair, width_here)
    keep = lax.dynamic_index_in_dim(halves, core, axis=1, keepdims=False)
    give = lax.dynamic_index_in_dim(halves, pair - 1 - core, axis=1, keepdims=False)
    swap = [(0, 1), (1, 0)]
    got = lax.ppermute(give, "core", swap)
    got_weights = partner_weights
    mine = (weights[:, None, None, None] * keep[None]).astype(jnp.bfloat16)
    theirs = (got_weights[:, None, None, None] * got[None]).astype(jnp.bfloat16)
    partial_sum = (mine.astype(jnp.float32) + theirs.astype(jnp.float32)).astype(jnp.bfloat16)
    summed = lax.psum_scatter(partial_sum, "z", scatter_dimension=1, tiled=True)
    summed = summed.reshape(3, GRID // chips // pair, width_here)
    return summed


def solution(mesh):
    chips = mesh.shape["freq"] // 2
    split = Mesh(mesh.devices.reshape(chips, 2, mesh.shape["row"]), ("z", "core", "row"))
    freq = ("z", "core")
    return jax.shard_map(
        shards,
        mesh=split,
        in_specs=(
            P(freq, "row", None, None),
            P(freq, "row", None, None),
            P(freq, "row", None, None),
            P(freq, "row", None),
            P(freq, "row", None),
            P(freq, "row", None),
            P(freq, "row"),
            P(),
        ),
        out_specs=P(None, freq, "row"),
        check_vma=False,
    )
```

```python
from functools import partial
import math

import jax
import jax.numpy as jnp
from jax import lax
from jax.sharding import Mesh, PartitionSpec as P
from jax.experimental import pallas as pl
from jax.experimental.pallas import tpu as pltpu

GRID = 4096
TU = 16
TV = 128


def for_sending(shard):
    return jax.tree.map(lambda a: a.astype(jnp.bfloat16) if a.dtype == jnp.float32 else a, shard)


def dft_tables(length):
    outer_len = 32
    inner_len = length // outer_len
    index_outer = jnp.arange(outer_len, dtype=jnp.int32)
    index_inner = jnp.arange(inner_len, dtype=jnp.int32)
    full_turn = 2.0 * math.pi
    angle_outer = (
        full_turn
        * (index_outer[:, None] * index_outer[None, :] % outer_len).astype(jnp.float32)
        / outer_len
    )
    angle_twist = (
        full_turn
        * (index_outer[:, None] * index_inner[None, :] % length).astype(jnp.float32)
        / length
    )
    angle_inner = (
        full_turn
        * (index_inner[:, None] * index_inner[None, :] % inner_len).astype(jnp.float32)
        / inner_len
    )
    return (
        jnp.cos(angle_outer),
        jnp.sin(angle_outer),
        jnp.cos(angle_twist),
        jnp.sin(angle_twist),
        jnp.cos(angle_inner),
        jnp.sin(angle_inner),
    )


def complex_weights(cos_part, sin_part, real_only=False):
    top = jnp.concatenate([cos_part, sin_part], axis=1)
    bottom = jnp.concatenate([-sin_part, cos_part], axis=1)
    if real_only:
        return jnp.stack([cos_part, -sin_part])
    return jnp.stack([top, bottom])


def transform_last(both):
    _, outer_len, row_total, inner_len = both.shape
    length = outer_len * inner_len
    cos_outer, sin_outer, cos_twist, sin_twist, cos_inner, sin_inner = dft_tables(length)
    product = partial(jnp.einsum, precision=lax.Precision.HIGH)
    step = product("parb,pak->krb", both, complex_weights(cos_outer, sin_outer))
    step_real = step[:outer_len]
    step_imag = step[outer_len:]
    twist_real = step_real * cos_twist[:, None, :] - step_imag * sin_twist[:, None, :]
    twist_imag = step_real * sin_twist[:, None, :] + step_imag * cos_twist[:, None, :]
    chunks = length // CHUNK
    weights = complex_weights(cos_inner, sin_inner).reshape(
        2, inner_len, 2, chunks, inner_len // chunks
    )
    out = product("qkrb,qbsdm->drsmk", jnp.stack([twist_real, twist_imag]), weights)
    return out.reshape(chunks, row_total, 2, CHUNK)


def transform_first_real(both):
    outer_len, inner_len, _, col_total = both.shape
    length = outer_len * inner_len
    cos_outer, sin_outer, cos_twist, sin_twist, cos_inner, sin_inner = dft_tables(length)
    product = partial(jnp.einsum, precision=lax.Precision.HIGH)
    step = product("abpc,pak->kbc", both, complex_weights(cos_outer, sin_outer))
    step_real = step[:outer_len]
    step_imag = step[outer_len:]
    twist_real = step_real * cos_twist[:, :, None] - step_imag * sin_twist[:, :, None]
    twist_imag = step_real * sin_twist[:, :, None] + step_imag * cos_twist[:, :, None]
    out_real = product(
        "qkbc,qbm->mkc",
        jnp.stack([twist_real, twist_imag]),
        complex_weights(cos_inner, sin_inner, real_only=True),
    )
    return out_real.reshape(length, col_total)


PAY_ROWS = 19
CHUNK = 128


GROUP = 16


def grid_kernel(tile_ref, pay_ref, out_ref, order_ref):
    tiles_total = out_ref.shape[2] // TU * out_ref.shape[1]
    tile_cols = out_ref.shape[1]
    lanes = pay_ref.shape[2]
    out_ref[...] = jnp.zeros(out_ref.shape, jnp.float32)
    du_base = lax.broadcasted_iota(jnp.int32, (TU, lanes), 0)
    dv_base = lax.broadcasted_iota(jnp.int32, (TV, lanes), 0).astype(jnp.bfloat16)

    def one_block(slot):
        blk = pay_ref[slot].astype(jnp.float32)
        vis = blk[0:2]
        ku = blk[2:9]
        ou = blk[16:17].astype(jnp.int32)
        du = du_base - ou
        su = jnp.zeros((TU, lanes), jnp.float32)
        for t in range(7):
            su = jnp.where(du == t, ku[t : t + 1], su)
        left = jnp.concatenate([vis[0:1] * su, vis[1:2] * su], axis=0).astype(jnp.bfloat16)
        raw = pay_ref[slot]
        dv = dv_base - raw[17:18]
        sv = jnp.zeros((TV, lanes), jnp.bfloat16)
        for t in range(7):
            sv = jnp.where(dv == t, raw[9 + t : 10 + t], sv)
        return lax.dot_general(
            left, sv, (((1,), (1,)), ((), ())), preferred_element_type=jnp.float32
        )

    def fill(s, filled):
        order_ref[filled] = s
        return filled + (tile_ref[s] < tiles_total).astype(jnp.int32)

    count = lax.fori_loop(0, pay_ref.shape[0], fill, jnp.int32(0))

    def body(i, carry):
        places = [i * GROUP + g for g in range(GROUP)]
        slots = [order_ref[jnp.minimum(q, count - 1)] for q in places]
        contribs = [one_block(s) for s in slots]
        for q, s, contrib in zip(places, slots, contribs):
            tile = jnp.minimum(tile_ref[s], tiles_total - 1)
            row0 = pl.multiple_of((tile // tile_cols) * TU, TU)
            col = tile % tile_cols

            @pl.when(q < count)
            def _():
                for p in range(2):
                    out_ref[p, col, pl.ds(row0, TU), :] += contrib[p * TU : (p + 1) * TU]
        return carry

    steps = (count + GROUP - 1) // GROUP
    lax.fori_loop(0, steps, body, 0)


def grid_into_slab(tile_ids, payload, slab_rows):
    return pl.pallas_call(
        grid_kernel,
        out_shape=jax.ShapeDtypeStruct((2, GRID // TV, slab_rows, TV), jnp.float32),
        in_specs=[
            pl.BlockSpec(memory_space=pltpu.SMEM),
            pl.BlockSpec(memory_space=pltpu.VMEM),
        ],
        out_specs=pl.BlockSpec(memory_space=pltpu.VMEM),
        scratch_shapes=[pltpu.SMEM((payload.shape[0],), jnp.int32)],
    )(tile_ids, payload)


def shards(
    vis_values, kernel_u, kernel_v, offset_u, offset_v, block_owner, tile_slot, channel_freq
):
    row_count = lax.axis_size("row")
    block_count = vis_values.shape[1]
    vis_count = vis_values.shape[3]
    capacity = max(2, 4 * block_count // row_count)
    slot_count = row_count * capacity
    slab_rows = GRID // row_count
    tiles_total = slab_rows // TU * (GRID // TV)
    owner_row = block_owner[0, :, 0]
    row_marks = (owner_row[:, None] == jnp.arange(row_count, dtype=jnp.int32)[None, :]).astype(
        jnp.int32
    )
    before = jnp.cumsum(row_marks, axis=0) - row_marks
    slot_rank = jnp.sum(before * row_marks, axis=1)
    target = owner_row * capacity + slot_rank
    tile_row = jnp.broadcast_to(
        tile_slot[0][:, None, None].astype(jnp.bfloat16), (block_count, 1, vis_count)
    )
    payload = jnp.concatenate(
        [
            vis_values[0],
            kernel_u[0],
            kernel_v[0],
            offset_u[0][:, None, :].astype(jnp.bfloat16),
            offset_v[0][:, None, :].astype(jnp.bfloat16),
            tile_row,
        ],
        axis=1,
    )
    pick = (target[None, :] == jnp.arange(slot_count, dtype=jnp.int32)[:, None]).astype(
        jnp.bfloat16
    )
    send = jnp.einsum(
        "sb,bkn->skn", pick, payload, preferred_element_type=jnp.float32
    )
    empty = 1.0 - jnp.sum(pick.astype(jnp.float32), axis=1)
    send = send.at[:, PAY_ROWS - 1, :].add(empty[:, None] * tiles_total)
    send = send.astype(jnp.bfloat16)
    recv = lax.all_to_all(
        send.reshape((row_count, capacity) + payload.shape[1:]),
        "row",
        split_axis=0,
        concat_axis=0,
        tiled=True,
    ).reshape((slot_count,) + payload.shape[1:])
    tile_ids = jnp.max(recv[:, PAY_ROWS - 1, :].astype(jnp.float32), axis=1).astype(jnp.int32)
    slab_grid = grid_into_slab(tile_ids, recv, slab_rows)
    spectrum = transform_last(slab_grid)
    image_scale = 1.0 / math.sqrt(block_count * row_count * vis_count)
    offset_freq = (channel_freq[0] - 1.284) / 0.428
    weights = jnp.stack([jnp.ones_like(offset_freq), offset_freq, offset_freq * offset_freq])
    received = lax.all_to_all(
        for_sending(spectrum), "row", split_axis=0, concat_axis=0, tiled=True
    ).astype(spectrum.dtype)
    width_here = received.shape[3]
    dirty_image = transform_first_real(received) * image_scale
    chips = lax.axis_size("z")
    pair = lax.axis_size("core")
    core = lax.axis_index("core")
    halves = dirty_image.reshape(chips, pair, GRID // chips // pair, width_here)
    keep = lax.dynamic_index_in_dim(halves, core, axis=1, keepdims=False)
    give = lax.dynamic_index_in_dim(halves, pair - 1 - core, axis=1, keepdims=False)
    swap = [(0, 1), (1, 0)]
    got = lax.ppermute(give, "core", swap)
    got_weights = lax.ppermute(weights, "core", swap)
    mine = (weights[:, None, None, None] * keep[None]).astype(jnp.bfloat16)
    theirs = (got_weights[:, None, None, None] * got[None]).astype(jnp.bfloat16)
    partial_sum = (mine.astype(jnp.float32) + theirs.astype(jnp.float32)).astype(jnp.bfloat16)
    summed = lax.psum_scatter(partial_sum, "z", scatter_dimension=1, tiled=True)
    summed = summed.reshape(3, GRID // chips // pair, width_here)
    return summed


def solution(mesh):
    chips = mesh.shape["freq"] // 2
    split = Mesh(mesh.devices.reshape(chips, 2, mesh.shape["row"]), ("z", "core", "row"))
    freq = ("z", "core")
    return jax.shard_map(
        shards,
        mesh=split,
        in_specs=(
            P(freq, "row", None, None),
            P(freq, "row", None, None),
            P(freq, "row", None, None),
            P(freq, "row", None),
            P(freq, "row", None),
            P(freq, "row", None),
            P(freq, "row"),
            P(freq),
        ),
        out_specs=P(None, freq, "row"),
        check_vma=False,
    )
```
